128 devices in a mesh: grp: 4 (over y_hi, core), blk: 32 (over x, z, y_lo).
Axes of the slice: x: 4, y: 4 (y_hi: 2, y_lo: 2; y = y_hi * 2 + y_lo), z: 4, core: 2. Of those that a mesh axis runs over, the one named last changes fastest.
Arguments:
- tokens: bfloat16 [16384, 2048], P(('grp', 'blk')), may hold values from -6 to 6
- expert_ids: int32 [16384, 6], P(('grp', 'blk')), may hold values from 0 to 7, all different within a row; in each aligned block of 128 rows (0 to 127, 128 to 255, ...) at most 128 rows name the same one
- gate_weights: float32 [16384, 6], P(('grp', 'blk')), may hold values from 0.1 to 1
- w_gate: bfloat16 [8, 1408, 2048], P('grp', 'blk'), may hold values from -0.125 to 0.125
- w_up: bfloat16 [8, 1408, 2048], P('grp', 'blk'), may hold values from -0.125 to 0.125
- w_down: bfloat16 [8, 1408, 2048], P('grp', 'blk'), may hold values from -0.15625 to 0.15625
Outputs:
- mixed: bfloat16 [16384, 2048], P(('grp', 'blk'))
The draws below stay inside these ranges and needn't reach their ends.
Inputs may be any that keep to these rules, and one draw needn't show every extreme that they name: `expert_ids`: each token names 6 different experts. Among the tokens of one device (aligned blocks of 128 tokens) no expert is named more than 128 times, a bound that some block reaches.
All inputs are finite; a program needn't handle non-finite values.
Results may differ from the reference program's by a relative error of at most 0.008.
Values may be sent and summed in bfloat16 or wider, within the bound.
No kernel may reach another device: no remote copies, remote signals or barrier semaphores. Data moves between devices by JAX's collectives and lax.ppermute only.
A program may use at most 128 MiB of HBM per device.

```python
import math
import jax
import jax.numpy as jnp
import numpy as np
from jax import lax

D = 2048
FF = 1408
TOP = 6
TOK_DEV = 128
CAP = 128
EXPERTS = 8
TOKENS = 16384


def level_of(stream_key, shape, split, low, high):
    factor_of, own = 1.0, jax.random.fold_in(stream_key, 6)
    for dim, parts in split:
        draws = jnp.exp(jax.random.uniform(jax.random.fold_in(own, dim), (parts,), jnp.float32, low / len(split), high / len(split)))
        factor_of = factor_of * jnp.repeat(draws, shape[dim] // parts).reshape([-1 if axis == dim else 1 for axis in range(len(shape))])
    return factor_of


def deal_out(key, own, number, rows, count, top, reach, skew):
    ranking = jax.random.permutation(key, count)
    crowded, common = portions_of(count, rows * top, reach, skew, True), portions_of(count, rows * top, reach, skew, False)
    places = jnp.arange(count)

    def named(lengths, rotation):
        used = int((lengths > 0).sum())
        fixed = max(1, used // 4)
        shifted = fixed + (places - fixed + rotation * (used - fixed)) % max(1, count - fixed)
        return jnp.zeros((count,), jnp.int32).at[ranking[jnp.where(places < fixed, places, shifted)]].set(jnp.asarray(lengths, jnp.int32))

    lengths = jnp.where(number % 4 == 0, named(crowded, number // 4), named(common, number - number // 4 - 1))
    mixed = jax.random.permutation(jax.random.fold_in(own, 3), count)
    giver, sink = mixed[0:count // 2 * 2:2], mixed[1:count // 2 * 2:2]
    room = jnp.minimum(lengths[giver] - 1, reach - lengths[sink]) // 2
    room = jnp.where((giver == ranking[0]) | (sink == ranking[0]) | (lengths[sink] == 0), 0, jnp.maximum(room, 0))
    shifted = jax.random.randint(jax.random.fold_in(own, 4), (count // 2,), 0, 1 << 20) % (room + 1)
    lengths = lengths.at[giver].add(-shifted).at[sink].add(shifted)
    labels = jnp.searchsorted(jnp.cumsum(lengths), jnp.arange(rows * top), side="right").astype(jnp.int32)
    table = labels.reshape(top, rows).T
    table = table[jax.random.permutation(jax.random.fold_in(own, 1), rows)]
    rotation = jax.random.randint(jax.random.fold_in(own, 2), (rows, 1), 0, top)
    return jnp.take_along_axis(table, (jnp.arange(top)[None, :] + rotation) % top, axis=1)


def portions_of(count, total, most, skew, full):
    weights = [(1 << 20) // math.isqrt(grade ** skew) + 1 for grade in range(1, count + 1)]
    largest = most if full else min(most, max(-(-total // count), total * weights[0] // sum(weights)))
    least = 1 if total - largest >= count - 1 else 0
    counts, spare = [largest] + [least] * (count - 1), total - largest - least * (count - 1)
    while spare > 0:
        candidates = [i for i in range(1, count) if counts[i] < largest] or [i for i in range(1, count) if counts[i] < most]
        whole, remaining = sum([weights[i] for i in candidates]), spare
        for i in candidates:
            more = min(most - counts[i], max(1, remaining * weights[i] // whole), spare)
            counts[i] = counts[i] + more
            spare = spare - more
    return np.array(counts)


def centred(own_key, extent, width, bound, split=(), kind=jnp.bfloat16):
    entries = width * jax.random.normal(own_key, extent, jnp.float32)
    if split:
        entries = entries * level_of(own_key, extent, split, -0.22, 0.18)
    return jnp.clip(entries, -bound, bound).astype(kind)


def setup_inputs(seed: int = 0) -> dict:
    streams_of = jax.random.split(jax.random.key(seed), 7)
    tokens = centred(streams_of[0], (TOKENS, D), 1.0, 6.0, ((0, 128),))
    expert_ids_keys = jax.random.split(jax.random.fold_in(streams_of[1], 1), TOKENS // TOK_DEV)
    expert_ids_turns = jax.random.permutation(jax.random.fold_in(streams_of[1], 3), TOKENS // TOK_DEV)
    expert_ids = jax.vmap(lambda own, number: deal_out(jax.random.fold_in(streams_of[1], 2), own, number, TOK_DEV, EXPERTS, TOP, CAP, 2))(expert_ids_keys, expert_ids_turns).reshape((TOKENS, TOP))
    gate_weights = jnp.clip(0.1 + 0.9 * jax.random.uniform(streams_of[2], (TOKENS, TOP), jnp.float32) ** level_of(streams_of[2], (TOKENS, TOP), ((0, 128),), -0.2, 0.2), 0.1, 1.0)
    w_gate = centred(streams_of[3], (EXPERTS, FF, D), D ** -0.5, 0.125, ((0, 4), (1, 32)))
    w_up = centred(streams_of[4], (EXPERTS, FF, D), D ** -0.5, 0.125, ((0, 4), (1, 32)))
    w_down = centred(streams_of[5], (EXPERTS, FF, D), FF ** -0.5, 0.15625, ((0, 4), (1, 32)))
    return dict(tokens=tokens, expert_ids=expert_ids, gate_weights=gate_weights, w_gate=w_gate, w_up=w_up, w_down=w_down)


def reference(tokens, expert_ids, gate_weights, w_gate, w_up, w_down):
    token_total = tokens.shape[0]
    top_count = expert_ids.shape[1]
    expert_total = w_gate.shape[0]
    flat_ids = expert_ids.reshape(-1)
    flat_gates = gate_weights.reshape(-1)
    pair_total = flat_ids.shape[0]
    capacity = (token_total // TOK_DEV) * CAP
    pair_index = jnp.arange(pair_total, dtype=jnp.int32)

    def one_expert(running, expert_weights):
        expert_id, gate_matrix, up_matrix, down_matrix = expert_weights
        chosen = flat_ids == expert_id
        position = jnp.cumsum(chosen.astype(jnp.int32)) - 1
        target = jnp.where(chosen, position, capacity).astype(jnp.int32)
        slot_owner = jnp.zeros((capacity,), jnp.int32).at[target].set(pair_index, mode="drop")
        slot_filled = jnp.zeros((capacity,), jnp.float32).at[target].set(1.0, mode="drop")
        token_of = (slot_owner // top_count).astype(jnp.int32)
        token_rows = tokens[token_of]
        gate_part = jnp.dot(token_rows, gate_matrix.T, preferred_element_type=jnp.float32)
        up_part = jnp.dot(token_rows, up_matrix.T, preferred_element_type=jnp.float32)
        hidden = (jax.nn.silu(gate_part) * up_part).astype(jnp.bfloat16)
        expert_out = jnp.dot(hidden, down_matrix, preferred_element_type=jnp.float32).astype(jnp.bfloat16)
        pair_weight = flat_gates[slot_owner] * slot_filled
        contribution = expert_out.astype(jnp.float32) * pair_weight[:, None]
        return running.at[token_of].add(contribution), None

    start_sum = jnp.zeros(tokens.shape, jnp.float32)
    expert_list = jnp.arange(expert_total, dtype=jnp.int32)
    running, _ = lax.scan(one_expert, start_sum, (expert_list, w_gate, w_up, w_down))
    return running.astype(jnp.bfloat16)
```

```python
import jax
import jax.numpy as jnp
from jax import lax
from jax.sharding import Mesh
from jax.sharding import PartitionSpec as P

POOL = ("grp", "ylo")
PLANE = ("x", "z")


def expert_weights(w, ylo):
    keep = lax.dynamic_index_in_dim(w, ylo, axis=0, keepdims=False)
    send = lax.dynamic_index_in_dim(w, 1 - ylo, axis=0, keepdims=False)
    got = lax.ppermute(send, "ylo", perm=[(0, 1), (1, 0)])
    pair = jnp.stack([keep, got])
    full = lax.all_gather(pair, PLANE, axis=0, tiled=False)
    return full.reshape(-1, w.shape[-1])


def per_device(tokens, expert_ids, gate_weights, w_gate, w_up, w_down):
    ylo = lax.axis_index("ylo")
    pool = lax.axis_size("grp") * lax.axis_size("ylo")
    me = lax.axis_index("grp") * lax.axis_size("ylo") + ylo
    token_count, model_width = tokens.shape

    gate_full = expert_weights(w_gate, ylo)
    up_full = expert_weights(w_up, ylo)
    down_full = expert_weights(w_down, ylo)

    rows = lax.all_gather(tokens, POOL, axis=0, tiled=True)
    gate_part = jnp.dot(rows, gate_full.T, preferred_element_type=jnp.float32)
    up_part = jnp.dot(rows, up_full.T, preferred_element_type=jnp.float32)
    hidden = (jax.nn.silu(gate_part) * up_part).astype(jnp.bfloat16)
    out = jnp.dot(hidden, down_full, preferred_element_type=jnp.float32).astype(jnp.bfloat16)

    back = lax.all_to_all(
        out.reshape(pool, token_count, model_width), POOL, split_axis=0, concat_axis=0, tiled=True
    )
    experts = jnp.arange(pool, dtype=jnp.int32)
    weight = jnp.sum(
        jnp.where(expert_ids[:, :, None] == experts[None, None, :], gate_weights[:, :, None], 0.0),
        axis=1,
    )
    del me
    mixed = jnp.einsum("te,etd->td", weight, back.astype(jnp.float32))
    return mixed.astype(jnp.bfloat16)


def solution(mesh):
    grp, blk = mesh.devices.shape
    ylo = 2
    fine = Mesh(
        mesh.devices.reshape(grp, 4, blk // (4 * ylo), ylo), ("grp", "x", "z", "ylo")
    )
    rows = P(("grp", "x", "z", "ylo"), None)
    weights = P("grp", ("x", "z", "ylo"), None)
    return jax.shard_map(
        per_device,
        mesh=fine,
        in_specs=(rows, rows, rows, weights, weights, weights),
        out_specs=rows,
        check_vma=False,
    )
```

```python
import jax
import jax.numpy as jnp
from jax import lax
from jax.sharding import Mesh
from jax.sharding import PartitionSpec as P

CHIPS = ("yhi", "ylo")
PLANE = ("x", "z")
SWAP = [(0, 1), (1, 0)]


def expert_weights(w, ylo):
    keep = lax.dynamic_index_in_dim(w, ylo, axis=0, keepdims=False)
    send = lax.dynamic_index_in_dim(w, 1 - ylo, axis=0, keepdims=False)
    got = lax.ppermute(send, "ylo", perm=SWAP)
    pair = jnp.stack([keep, got])
    full = lax.all_gather(pair, PLANE, axis=0, tiled=False)
    return full.reshape(-1, w.shape[-1])


def spread(value, chips):
    sent = jnp.broadcast_to(value[None], (chips,) + value.shape)
    mine = lax.all_to_all(sent, CHIPS, split_axis=0, concat_axis=0, tiled=True)
    other = lax.ppermute(mine, "core", perm=SWAP)
    return mine, other


def per_device(tokens, expert_ids, gate_weights, w_gate, w_up, w_down):
    ylo = lax.axis_index("ylo")
    chips = lax.axis_size("yhi") * lax.axis_size("ylo")
    expert = (lax.axis_index("yhi") * lax.axis_size("core") + lax.axis_index("core")) * 2 + ylo
    token_count, model_width = tokens.shape

    gate_full = expert_weights(w_gate, ylo)
    up_full = expert_weights(w_up, ylo)
    down_full = expert_weights(w_down, ylo)

    experts = jnp.arange(lax.axis_size("core") * chips, dtype=jnp.int32)
    weight = jnp.sum(
        jnp.where(expert_ids[:, :, None] == experts, gate_weights[:, :, None], 0.0), axis=1
    )
    rows_mine, rows_other = spread(tokens, chips)
    weight_mine, weight_other = spread(weight, chips)
    rows = jnp.concatenate([rows_mine, rows_other]).reshape(-1, model_width)
    table = jnp.concatenate([weight_mine, weight_other]).reshape(-1, experts.shape[0])
    scale = lax.dynamic_index_in_dim(table, expert, axis=1, keepdims=True)

    gate_part = jnp.dot(rows, gate_full.T, preferred_element_type=jnp.float32)
    up_part = jnp.dot(rows, up_full.T, preferred_element_type=jnp.float32)
    hidden = (jax.nn.silu(gate_part) * up_part).astype(jnp.bfloat16)
    out = jnp.dot(hidden, down_full, preferred_element_type=jnp.float32).astype(jnp.bfloat16)
    scaled = (out.astype(jnp.float32) * scale).reshape(2, chips, token_count, model_width)

    partner = lax.ppermute(scaled[1], "core", perm=SWAP)
    partial = (scaled[0] + partner).astype(jnp.bfloat16)
    back = lax.all_to_all(partial, CHIPS, split_axis=0, concat_axis=0, tiled=True)
    mixed = jnp.sum(back.astype(jnp.float32), axis=0)
    return mixed.astype(jnp.bfloat16)


def solution(mesh):
    grp, blk = mesh.devices.shape
    ylo = 2
    fine = Mesh(
        mesh.devices.reshape(2, grp // 2, 4, blk // (4 * ylo), ylo),
        ("yhi", "core", "x", "z", "ylo"),
    )
    rows = P(("yhi", "core", "x", "z", "ylo"), None)
    weights = P(("yhi", "core"), ("x", "z", "ylo"), None)
    return jax.shard_map(
        per_device,
        mesh=fine,
        in_specs=(rows, rows, rows, weights, weights, weights),
        out_specs=rows,
        check_vma=False,
    )
```

```python
import jax
import jax.numpy as jnp
from jax import lax
from jax.sharding import Mesh
from jax.sharding import PartitionSpec as P

CHIPS = ("yhi", "ylo")
PLANE = ("x", "z")
SWAP = [(0, 1), (1, 0)]


def expert_weights(w, ylo, by_permutes=False):
    keep = lax.dynamic_index_in_dim(w, ylo, axis=0, keepdims=False)
    send = lax.dynamic_index_in_dim(w, 1 - ylo, axis=0, keepdims=False)
    got = lax.ppermute(send, "ylo", perm=SWAP)
    pair = jnp.stack([keep, got])
    if by_permutes:
        full = plane_by_permutes(pair)
    else:
        full = lax.all_gather(pair, PLANE, axis=0, tiled=False)
    return full.reshape(-1, w.shape[-1])


def ring_of_four(value, axis):
    ahead = [(i, (i + 1) % 4) for i in range(4)]
    behind = [(i, (i - 1) % 4) for i in range(4)]
    from_minus = lax.ppermute(value, axis, perm=ahead)
    from_plus = lax.ppermute(value, axis, perm=behind)
    half = value.shape[-1] // 2
    far = jnp.concatenate(
        [
            lax.ppermute(from_minus[..., :half], axis, perm=ahead),
            lax.ppermute(from_plus[..., half:], axis, perm=behind),
        ],
        axis=-1,
    )
    relative = jnp.stack([value, from_plus, far, from_minus])
    return jnp.roll(relative, lax.axis_index(axis), axis=0)


def plane_by_permutes(pair):
    half = pair.shape[-1] // 2
    z_first = ring_of_four(ring_of_four(pair[..., :half], "z"), "x")
    x_first = ring_of_four(ring_of_four(pair[..., half:], "x"), "z")
    x_first = jnp.swapaxes(x_first, 0, 1)
    return jnp.concatenate([z_first, x_first], axis=-1)


def spread(value, chips):
    sent = jnp.broadcast_to(value[None], (chips,) + value.shape)
    mine = lax.all_to_all(sent, CHIPS, split_axis=0, concat_axis=0, tiled=True)
    other = lax.ppermute(mine, "core", perm=SWAP)
    return mine, other


def per_device(tokens, expert_ids, gate_weights, w_gate, w_up, w_down):
    ylo = lax.axis_index("ylo")
    chips = lax.axis_size("yhi") * lax.axis_size("ylo")
    expert = (lax.axis_index("yhi") * lax.axis_size("core") + lax.axis_index("core")) * 2 + ylo
    token_count, model_width = tokens.shape

    gate_full = expert_weights(w_gate, ylo)
    up_full = expert_weights(w_up, ylo)
    down_full = expert_weights(w_down, ylo, by_permutes=True)

    experts = jnp.arange(lax.axis_size("core") * chips, dtype=jnp.int32)
    weight = jnp.sum(
        jnp.where(expert_ids[:, :, None] == experts, gate_weights[:, :, None], 0.0), axis=1
    )
    rows_mine, rows_other = spread(tokens, chips)
    weight_mine, weight_other = spread(weight, chips)
    rows = jnp.concatenate([rows_mine, rows_other]).reshape(-1, model_width)
    table = jnp.concatenate([weight_mine, weight_other]).reshape(-1, experts.shape[0])
    scale = lax.dynamic_index_in_dim(table, expert, axis=1, keepdims=True)

    gate_part = jnp.dot(rows, gate_full.T, preferred_element_type=jnp.float32)
    up_part = jnp.dot(rows, up_full.T, preferred_element_type=jnp.float32)
    hidden = (jax.nn.silu(gate_part) * up_part).astype(jnp.bfloat16)
    out = jnp.dot(hidden, down_full, preferred_element_type=jnp.float32).astype(jnp.bfloat16)
    scaled = (out.astype(jnp.float32) * scale).reshape(2, chips, token_count, model_width)

    partner = lax.ppermute(scaled[1], "core", perm=SWAP)
    partial = (scaled[0] + partner).astype(jnp.bfloat16)
    back = lax.all_to_all(partial, CHIPS, split_axis=0, concat_axis=0, tiled=True)
    mixed = jnp.sum(back.astype(jnp.float32), axis=0)
    return mixed.astype(jnp.bfloat16)


def solution(mesh):
    grp, blk = mesh.devices.shape
    ylo = 2
    fine = Mesh(
        mesh.devices.reshape(2, grp // 2, 4, blk // (4 * ylo), ylo),
        ("yhi", "core", "x", "z", "ylo"),
    )
    rows = P(("yhi", "core", "x", "z", "ylo"), None)
    weights = P(("yhi", "core"), ("x", "z", "ylo"), None)
    return jax.shard_map(
        per_device,
        mesh=fine,
        in_specs=(rows, rows, rows, weights, weights, weights),
        out_specs=rows,
        check_vma=False,
    )
```

```python
import jax
import jax.numpy as jnp
from jax import lax
from jax.sharding import Mesh
from jax.sharding import PartitionSpec as P

CHIPS = ("yhi", "ylo")
SWAP = [(0, 1), (1, 0)]


def ring_of_four(value, axis):
    ahead = [(i, (i + 1) % 4) for i in range(4)]
    behind = [(i, (i - 1) % 4) for i in range(4)]
    from_minus = lax.ppermute(value, axis, perm=ahead)
    from_plus = lax.ppermute(value, axis, perm=behind)
    half = value.shape[-1] // 2
    far = jnp.concatenate(
        [
            lax.ppermute(from_minus[..., :half], axis, perm=ahead),
            lax.ppermute(from_plus[..., half:], axis, perm=behind),
        ],
        axis=-1,
    )
    return jnp.stack([value, from_plus, far, from_minus])


def expert_weights(w_gate, w_up, w_down, ylo):
    stacked = jnp.stack([w_gate, w_up, w_down], axis=1)
    rows = stacked.shape[2]
    padded = -(-rows // 16) * 16
    stacked = jnp.pad(stacked, ((0, 0), (0, 0), (0, padded - rows), (0, 0)))
    keep = lax.dynamic_index_in_dim(stacked, ylo, axis=0, keepdims=False)
    send = lax.dynamic_index_in_dim(stacked, 1 - ylo, axis=0, keepdims=False)
    got = lax.ppermute(send, "ylo", perm=SWAP)
    set_a = ring_of_four(ring_of_four(keep, "z"), "x")
    set_b = ring_of_four(ring_of_four(got, "x"), "z")
    width = stacked.shape[-1]
    return [
        jnp.moveaxis(part, 2, 0).reshape(3, -1, width) for part in (set_a, set_b)
    ]


def spread(value, chips):
    sent = jnp.broadcast_to(value[None], (chips,) + value.shape)
    mine = lax.all_to_all(sent, CHIPS, split_axis=0, concat_axis=0, tiled=True)
    other = lax.ppermute(mine, "core", perm=SWAP)
    return mine, other


def per_device(tokens, expert_ids, gate_weights, w_gate, w_up, w_down):
    ylo = lax.axis_index("ylo")
    chips = lax.axis_size("yhi") * lax.axis_size("ylo")
    expert = (lax.axis_index("yhi") * lax.axis_size("core") + lax.axis_index("core")) * 2 + ylo
    token_count, model_width = tokens.shape

    sets = expert_weights(w_gate, w_up, w_down, ylo)

    experts = jnp.arange(lax.axis_size("core") * chips, dtype=jnp.int32)
    weight = jnp.sum(
        jnp.where(expert_ids[:, :, None] == experts, gate_weights[:, :, None], 0.0), axis=1
    )
    rows_mine, rows_other = spread(tokens, chips)
    weight_mine, weight_other = spread(weight, chips)
    rows = jnp.concatenate([rows_mine, rows_other]).reshape(-1, model_width)
    table = jnp.concatenate([weight_mine, weight_other]).reshape(-1, experts.shape[0])
    scale = lax.dynamic_index_in_dim(table, expert, axis=1, keepdims=True)

    out = None
    for weights in sets:
        gate_part = jnp.dot(rows, weights[0].T, preferred_element_type=jnp.float32)
        up_part = jnp.dot(rows, weights[1].T, preferred_element_type=jnp.float32)
        hidden = (jax.nn.silu(gate_part) * up_part).astype(jnp.bfloat16)
        part = jnp.dot(hidden, weights[2], preferred_element_type=jnp.float32)
        out = part if out is None else out + part
    out = out.astype(jnp.bfloat16)
    scaled = (out.astype(jnp.float32) * scale).reshape(2, chips, token_count, model_width)

    partner = lax.ppermute(scaled[1], "core", perm=SWAP)
    partial = (scaled[0] + partner).astype(jnp.bfloat16)
    back = lax.all_to_all(partial, CHIPS, split_axis=0, concat_axis=0, tiled=True)
    mixed = jnp.sum(back.astype(jnp.float32), axis=0)
    return mixed.astype(jnp.bfloat16)


def solution(mesh):
    grp, blk = mesh.devices.shape
    ylo = 2
    fine = Mesh(
        mesh.devices.reshape(2, grp // 2, 4, blk // (4 * ylo), ylo),
        ("yhi", "core", "x", "z", "ylo"),
    )
    rows = P(("yhi", "core", "x", "z", "ylo"), None)
    weights = P(("yhi", "core"), ("x", "z", "ylo"), None)
    return jax.shard_map(
        per_device,
        mesh=fine,
        in_specs=(rows, rows, rows, weights, weights, weights),
        out_specs=rows,
        check_vma=False,
    )
```

```python
import jax
import jax.numpy as jnp
from jax import lax
from jax.sharding import Mesh
from jax.sharding import PartitionSpec as P

CHIPS = ("yhi", "ylo")
SWAP = [(0, 1), (1, 0)]


def ring_of_four(value, axis):
    ahead = [(i, (i + 1) % 4) for i in range(4)]
    behind = [(i, (i - 1) % 4) for i in range(4)]
    from_minus = lax.ppermute(value, axis, perm=ahead)
    from_plus = lax.ppermute(value, axis, perm=behind)
    half = value.shape[-1] // 2
    far = jnp.concatenate(
        [
            lax.ppermute(from_minus[..., :half], axis, perm=ahead),
            lax.ppermute(from_plus[..., half:], axis, perm=behind),
        ],
        axis=-1,
    )
    return jnp.stack([value, from_plus, far, from_minus])


def expert_weights(w_gate, w_up, w_down, ylo):
    stacked = jnp.stack([w_gate, w_up, w_down], axis=1)
    rows = stacked.shape[2]
    padded = -(-rows // 16) * 16
    stacked = jnp.pad(stacked, ((0, 0), (0, 0), (0, padded - rows), (0, 0)))
    keep = lax.dynamic_index_in_dim(stacked, ylo, axis=0, keepdims=False)
    send = lax.dynamic_index_in_dim(stacked, 1 - ylo, axis=0, keepdims=False)
    got = lax.ppermute(send, "ylo", perm=SWAP)
    first_a = ring_of_four(keep, "z")
    first_b = ring_of_four(got, "x")
    first_a, first_b = lax.optimization_barrier((first_a, first_b))
    gate_up_a = ring_of_four(first_a[:, :2], "x")
    gate_up_b = ring_of_four(first_b[:, :2], "z")
    gate_up_a, gate_up_b, down_a, down_b = lax.optimization_barrier(
        (gate_up_a, gate_up_b, first_a[:, 2], first_b[:, 2])
    )
    down_a = ring_of_four(down_a, "x")
    down_b = ring_of_four(down_b, "z")
    width = stacked.shape[-1]
    sets = []
    for gate_up, down in ((gate_up_a, down_a), (gate_up_b, down_b)):
        gate_up = jnp.moveaxis(gate_up, 2, 0).reshape(2, -1, width)
        sets.append((gate_up[0], gate_up[1], down.reshape(-1, width)))
    return sets


def spread(value, chips):
    sent = jnp.broadcast_to(value[None], (chips,) + value.shape)
    mine = lax.all_to_all(sent, CHIPS, split_axis=0, concat_axis=0, tiled=True)
    other = lax.ppermute(mine, "core", perm=SWAP)
    return mine, other


def per_device(tokens, expert_ids, gate_weights, w_gate, w_up, w_down):
    ylo = lax.axis_index("ylo")
    chips = lax.axis_size("yhi") * lax.axis_size("ylo")
    expert = (lax.axis_index("yhi") * lax.axis_size("core") + lax.axis_index("core")) * 2 + ylo
    token_count, model_width = tokens.shape

    sets = expert_weights(w_gate, w_up, w_down, ylo)

    experts = jnp.arange(lax.axis_size("core") * chips, dtype=jnp.int32)
    weight = jnp.sum(
        jnp.where(expert_ids[:, :, None] == experts, gate_weights[:, :, None], 0.0), axis=1
    )
    rows_mine, rows_other = spread(tokens, chips)
    weight_mine, weight_other = spread(weight, chips)
    rows = jnp.concatenate([rows_mine, rows_other]).reshape(-1, model_width)
    table = jnp.concatenate([weight_mine, weight_other]).reshape(-1, experts.shape[0])
    scale = lax.dynamic_index_in_dim(table, expert, axis=1, keepdims=True)

    out = None
    for weights in sets:
        gate_part = jnp.dot(rows, weights[0].T, preferred_element_type=jnp.float32)
        up_part = jnp.dot(rows, weights[1].T, preferred_element_type=jnp.float32)
        hidden = (jax.nn.silu(gate_part) * up_part).astype(jnp.bfloat16)
        part = jnp.dot(hidden, weights[2], preferred_element_type=jnp.float32)
        out = part if out is None else out + part
    out = out.astype(jnp.bfloat16)
    scaled = (out.astype(jnp.float32) * scale).reshape(2, chips, token_count, model_width)

    partner = lax.ppermute(scaled[1], "core", perm=SWAP)
    partial = (scaled[0] + partner).astype(jnp.bfloat16)
    back = lax.all_to_all(partial, CHIPS, split_axis=0, concat_axis=0, tiled=True)
    mixed = jnp.sum(back.astype(jnp.float32), axis=0)
    return mixed.astype(jnp.bfloat16)


def solution(mesh):
    grp, blk = mesh.devices.shape
    ylo = 2
    fine = Mesh(
        mesh.devices.reshape(2, grp // 2, 4, blk // (4 * ylo), ylo),
        ("yhi", "core", "x", "z", "ylo"),
    )
    rows = P(("yhi", "core", "x", "z", "ylo"), None)
    weights = P(("yhi", "core"), ("x", "z", "ylo"), None)
    return jax.shard_map(
        per_device,
        mesh=fine,
        in_specs=(rows, rows, rows, weights, weights, weights),
        out_specs=rows,
        check_vma=False,
    )
```

```python
import jax
import jax.numpy as jnp
from jax import lax
from jax.sharding import Mesh
from jax.sharding import PartitionSpec as P

CHIPS = ("yhi", "ylo")
SWAP = [(0, 1), (1, 0)]


def ring_of_four(value, axis):
    ahead = [(i, (i + 1) % 4) for i in range(4)]
    behind = [(i, (i - 1) % 4) for i in range(4)]
    from_minus = lax.ppermute(value, axis, perm=ahead)
    from_plus = lax.ppermute(value, axis, perm=behind)
    half = value.shape[-1] // 2
    far = jnp.concatenate(
        [
            lax.ppermute(from_minus[..., :half], axis, perm=ahead),
            lax.ppermute(from_plus[..., half:], axis, perm=behind),
        ],
        axis=-1,
    )
    return jnp.stack([value, from_plus, far, from_minus])


def expert_weights(w_gate, w_up, w_down, ylo):
    stacked = jnp.stack([w_gate, w_up, w_down], axis=1)
    rows = stacked.shape[2]
    padded = -(-rows // 16) * 16
    stacked = jnp.pad(stacked, ((0, 0), (0, 0), (0, padded - rows), (0, 0)))
    keep = lax.dynamic_index_in_dim(stacked, ylo, axis=0, keepdims=False)
    send = lax.dynamic_index_in_dim(stacked, 1 - ylo, axis=0, keepdims=False)
    got = lax.ppermute(send, "ylo", perm=SWAP)
    first_a = ring_of_four(keep, "z")
    first_b = ring_of_four(got, "x")
    first_a, first_b = lax.optimization_barrier((first_a, first_b))
    gate_up_a = ring_of_four(first_a[:, :2], "x")
    gate_up_b = ring_of_four(first_b[:, :2], "z")
    gate_up_a, gate_up_b, down_a, down_b = lax.optimization_barrier(
        (gate_up_a, gate_up_b, first_a[:, 2], first_b[:, 2])
    )
    down_a = ring_of_four(down_a, "x")
    down_b = ring_of_four(down_b, "z")
    width = stacked.shape[-1]
    sets = []
    for gate_up, down in ((gate_up_a, down_a), (gate_up_b, down_b)):
        gate_up = jnp.moveaxis(gate_up, 2, 0).reshape(2, -1, width)
        sets.append((gate_up[0], gate_up[1], down.reshape(-1, width)))
    return sets


def spread(value):
    mine = lax.all_gather(value, CHIPS, axis=0, tiled=False)
    other = lax.ppermute(mine, "core", perm=SWAP)
    return mine, other


def per_device(tokens, expert_ids, gate_weights, w_gate, w_up, w_down):
    ylo = lax.axis_index("ylo")
    chips = lax.axis_size("yhi") * lax.axis_size("ylo")
    expert = (lax.axis_index("yhi") * lax.axis_size("core") + lax.axis_index("core")) * 2 + ylo
    token_count, model_width = tokens.shape

    sets = expert_weights(w_gate, w_up, w_down, ylo)

    experts = jnp.arange(lax.axis_size("core") * chips, dtype=jnp.int32)
    weight = jnp.sum(
        jnp.where(expert_ids[:, :, None] == experts, gate_weights[:, :, None], 0.0), axis=1
    )
    rows_mine, rows_other = spread(tokens)
    weight_mine, weight_other = spread(weight)
    rows = jnp.concatenate([rows_mine, rows_other]).reshape(-1, model_width)
    table = jnp.concatenate([weight_mine, weight_other]).reshape(-1, experts.shape[0])
    scale = lax.dynamic_index_in_dim(table, expert, axis=1, keepdims=True)

    out = None
    for weights in sets:
        gate_part = jnp.dot(rows, weights[0].T, preferred_element_type=jnp.float32)
        up_part = jnp.dot(rows, weights[1].T, preferred_element_type=jnp.float32)
        hidden = (jax.nn.silu(gate_part) * up_part).astype(jnp.bfloat16)
        part = jnp.dot(hidden, weights[2], preferred_element_type=jnp.float32)
        out = part if out is None else out + part
    out = out.astype(jnp.bfloat16)
    scaled = (out.astype(jnp.float32) * scale).reshape(2, chips, token_count, model_width)

    partner = lax.ppermute(scaled[1], "core", perm=SWAP)
    partial = (scaled[0] + partner).astype(jnp.bfloat16)
    back = lax.all_to_all(partial, CHIPS, split_axis=0, concat_axis=0, tiled=True)
    mixed = jnp.sum(back.astype(jnp.float32), axis=0)
    return mixed.astype(jnp.bfloat16)


def solution(mesh):
    grp, blk = mesh.devices.shape
    ylo = 2
    fine = Mesh(
        mesh.devices.reshape(2, grp // 2, 4, blk // (4 * ylo), ylo),
        ("yhi", "core", "x", "z", "ylo"),
    )
    rows = P(("yhi", "core", "x", "z", "ylo"), None)
    weights = P(("yhi", "core"), ("x", "z", "ylo"), None)
    return jax.shard_map(
        per_device,
        mesh=fine,
        in_specs=(rows, rows, rows, weights, weights, weights),
        out_specs=rows,
        check_vma=False,
    )
```

```python
import jax
import jax.numpy as jnp
from jax import lax
from jax.sharding import Mesh
from jax.sharding import PartitionSpec as P

CHIPS = ("yhi", "ylo")
SWAP = [(0, 1), (1, 0)]


def ring_of_four(value, axis):
    ahead = [(i, (i + 1) % 4) for i in range(4)]
    behind = [(i, (i - 1) % 4) for i in range(4)]
    from_minus = lax.ppermute(value, axis, perm=ahead)
    from_plus = lax.ppermute(value, axis, perm=behind)
    half = value.shape[-1] // 2
    far = jnp.concatenate(
        [
            lax.ppermute(from_minus[..., :half], axis, perm=ahead),
            lax.ppermute(from_plus[..., half:], axis, perm=behind),
        ],
        axis=-1,
    )
    return jnp.stack([value, from_plus, far, from_minus])


def expert_weights(w_gate, w_up, w_down, ylo):
    stacked = jnp.stack([w_gate, w_up, w_down], axis=1)
    rows = stacked.shape[2]
    padded = -(-rows // 16) * 16
    stacked = jnp.pad(stacked, ((0, 0), (0, 0), (0, padded - rows), (0, 0)))
    keep = lax.dynamic_index_in_dim(stacked, ylo, axis=0, keepdims=False)
    send = lax.dynamic_index_in_dim(stacked, 1 - ylo, axis=0, keepdims=False)
    got = lax.ppermute(send, "ylo", perm=SWAP)
    first_a = ring_of_four(keep, "z")
    first_b = ring_of_four(got, "x")
    first_a, first_b = lax.optimization_barrier((first_a, first_b))
    gate_up_a = ring_of_four(first_a[:, :2], "x")
    gate_up_b = ring_of_four(first_b[:, :2], "z")
    gate_up_a, gate_up_b, down_a, down_b = lax.optimization_barrier(
        (gate_up_a, gate_up_b, first_a[:, 2], first_b[:, 2])
    )
    down_a = ring_of_four(down_a, "x")
    down_b = ring_of_four(down_b, "z")
    width = stacked.shape[-1]
    sets = []
    for gate_up, down in ((gate_up_a, down_a), (gate_up_b, down_b)):
        gate_up = jnp.moveaxis(gate_up, 2, 0).reshape(2, -1, width)
        sets.append((gate_up[0], gate_up[1], down.reshape(-1, width)))
    return sets


def spread(value, chips):
    sent = jnp.broadcast_to(value[None], (chips,) + value.shape)
    mine = lax.all_to_all(sent, CHIPS, split_axis=0, concat_axis=0, tiled=True)
    other = lax.ppermute(mine, "core", perm=SWAP)
    return mine, other


def per_device(tokens, expert_ids, gate_weights, w_gate, w_up, w_down):
    ylo = lax.axis_index("ylo")
    chips = lax.axis_size("yhi") * lax.axis_size("ylo")
    expert = (lax.axis_index("yhi") * lax.axis_size("core") + lax.axis_index("core")) * 2 + ylo
    token_count, model_width = tokens.shape

    sets = expert_weights(w_gate, w_up, w_down, ylo)

    experts = jnp.arange(lax.axis_size("core") * chips, dtype=jnp.int32)
    weight = jnp.sum(
        jnp.where(expert_ids[:, :, None] == experts, gate_weights[:, :, None], 0.0), axis=1
    )
    rows_mine, rows_other = spread(tokens, chips)
    weight_mine, weight_other = spread(weight, chips)
    scale_mine = lax.dynamic_index_in_dim(weight_mine, expert, axis=2, keepdims=False)
    scale_other = lax.dynamic_index_in_dim(weight_other, expert, axis=2, keepdims=False)
    chip = lax.axis_index("yhi") * lax.axis_size("ylo") + ylo

    offsets = (2, 1, 3, 0)
    chunks = []
    for offset in offsets:
        dest = (chip + offset) % chips
        rows = jnp.concatenate(
            [
                lax.dynamic_index_in_dim(rows_mine, dest, keepdims=False),
                lax.dynamic_index_in_dim(rows_other, dest, keepdims=False),
            ]
        )
        scale = jnp.concatenate(
            [
                lax.dynamic_index_in_dim(scale_mine, dest, keepdims=False),
                lax.dynamic_index_in_dim(scale_other, dest, keepdims=False),
            ]
        )
        hiddens = []
        for weights in sets:
            gate_part = jnp.dot(rows, weights[0].T, preferred_element_type=jnp.float32)
            up_part = jnp.dot(rows, weights[1].T, preferred_element_type=jnp.float32)
            hiddens.append((jax.nn.silu(gate_part) * up_part).astype(jnp.bfloat16))
        chunks.append((hiddens, scale))

    def send(partial, offset):
        if offset:
            ring = [(i, (i + offset) % chips) for i in range(chips)]
            partial = lax.ppermute(partial, CHIPS, perm=ring)
        return partial.astype(jnp.float32)

    received = []
    pending = None
    for offset, (hiddens, scale) in zip(offsets, chunks):
        if pending is not None:
            tied = [pending[0]] + received[-1:]
            hiddens, tied = lax.optimization_barrier((hiddens, tied))
            received[-1:] = tied[1:]
            received.append(send(tied[0], pending[1]))
        out = None
        for hidden, weights in zip(hiddens, sets):
            part = jnp.dot(hidden, weights[2], preferred_element_type=jnp.float32)
            out = part if out is None else out + part
        scaled = out.astype(jnp.bfloat16).astype(jnp.float32) * scale[:, None]
        partner = lax.ppermute(scaled[token_count:], "core", perm=SWAP)
        pending = ((scaled[:token_count] + partner).astype(jnp.bfloat16), offset)
    received.append(send(*pending))
    mixed = received[0]
    for got in received[1:]:
        mixed = mixed + got
    return mixed.astype(jnp.bfloat16)


def solution(mesh):
    grp, blk = mesh.devices.shape
    ylo = 2
    fine = Mesh(
        mesh.devices.reshape(2, grp // 2, 4, blk // (4 * ylo), ylo),
        ("yhi", "core", "x", "z", "ylo"),
    )
    rows = P(("yhi", "core", "x", "z", "ylo"), None)
    weights = P(("yhi", "core"), ("x", "z", "ylo"), None)
    return jax.shard_map(
        per_device,
        mesh=fine,
        in_specs=(rows, rows, rows, weights, weights, weights),
        out_specs=rows,
        check_vma=False,
    )
```

```python
import jax
import jax.numpy as jnp
from jax import lax
from jax.sharding import Mesh
from jax.sharding import PartitionSpec as P

CHIPS = ("yhi", "ylo")
SWAP = [(0, 1), (1, 0)]


def ring_of_four(value, axis):
    ahead = [(i, (i + 1) % 4) for i in range(4)]
    behind = [(i, (i - 1) % 4) for i in range(4)]
    from_minus = lax.ppermute(value, axis, perm=ahead)
    from_plus = lax.ppermute(value, axis, perm=behind)
    half = value.shape[-1] // 2
    far = jnp.concatenate(
        [
            lax.ppermute(from_minus[..., :half], axis, perm=ahead),
            lax.ppermute(from_plus[..., half:], axis, perm=behind),
        ],
        axis=-1,
    )
    return jnp.stack([value, from_plus, far, from_minus])


def expert_weights(w_gate, w_up, w_down, ylo):
    stacked = jnp.stack([w_gate, w_up, w_down], axis=1)
    rows = stacked.shape[2]
    padded = -(-rows // 16) * 16
    stacked = jnp.pad(stacked, ((0, 0), (0, 0), (0, padded - rows), (0, 0)))
    keep = lax.dynamic_index_in_dim(stacked, ylo, axis=0, keepdims=False)
    send = lax.dynamic_index_in_dim(stacked, 1 - ylo, axis=0, keepdims=False)
    got = lax.ppermute(send, "ylo", perm=SWAP)
    first_a = ring_of_four(keep, "z")
    first_b = ring_of_four(got, "x")
    first_a, first_b = lax.optimization_barrier((first_a, first_b))
    gate_up_a = ring_of_four(first_a[:, :2], "x")
    gate_up_b = ring_of_four(first_b[:, :2], "z")
    gate_up_a, gate_up_b, down_a, down_b = lax.optimization_barrier(
        (gate_up_a, gate_up_b, first_a[:, 2], first_b[:, 2])
    )
    down_a = ring_of_four(down_a, "x")
    down_b = ring_of_four(down_b, "z")
    width = stacked.shape[-1]
    sets = []
    for gate_up, down in ((gate_up_a, down_a), (gate_up_b, down_b)):
        gate_up = jnp.moveaxis(gate_up, 2, 0).reshape(2, -1, width)
        sets.append((gate_up[0], gate_up[1], down.reshape(-1, width)))
    return sets


def spread(value, chips):
    sent = jnp.broadcast_to(value[None], (chips,) + value.shape)
    mine = lax.all_to_all(sent, CHIPS, split_axis=0, concat_axis=0, tiled=True)
    other = lax.ppermute(mine, "core", perm=SWAP)
    return mine, other


def per_device(tokens, expert_ids, gate_weights, w_gate, w_up, w_down):
    ylo = lax.axis_index("ylo")
    chips = lax.axis_size("yhi") * lax.axis_size("ylo")
    expert = (lax.axis_index("yhi") * lax.axis_size("core") + lax.axis_index("core")) * 2 + ylo
    token_count, model_width = tokens.shape

    sets = expert_weights(w_gate, w_up, w_down, ylo)

    experts = jnp.arange(lax.axis_size("core") * chips, dtype=jnp.int32)
    weight = jnp.sum(
        jnp.where(expert_ids[:, :, None] == experts, gate_weights[:, :, None], 0.0), axis=1
    )
    high = weight.astype(jnp.bfloat16)
    low = (weight - high.astype(jnp.float32)).astype(jnp.bfloat16)
    packed = jnp.concatenate([high, low], axis=1).reshape(-1, model_width)
    extra = packed.shape[0]
    packed = jnp.pad(packed, ((0, 16 - extra), (0, 0)))
    mine, other = spread(jnp.concatenate([tokens, packed]), chips)
    both = jnp.concatenate([mine, other])
    rows = both[:, :token_count].reshape(-1, model_width)
    halves = both[:, token_count:token_count + extra].reshape(-1, 2, experts.shape[0])
    table = halves[:, 0].astype(jnp.float32) + halves[:, 1].astype(jnp.float32)
    scale = lax.dynamic_index_in_dim(table, expert, axis=1, keepdims=True)

    out = None
    for weights in sets:
        gate_part = jnp.dot(rows, weights[0].T, preferred_element_type=jnp.float32)
        up_part = jnp.dot(rows, weights[1].T, preferred_element_type=jnp.float32)
        hidden = (jax.nn.silu(gate_part) * up_part).astype(jnp.bfloat16)
        part = jnp.dot(hidden, weights[2], preferred_element_type=jnp.float32)
        out = part if out is None else out + part
    out = out.astype(jnp.bfloat16)
    scaled = (out.astype(jnp.float32) * scale).reshape(2, chips, token_count, model_width)

    partner = lax.ppermute(scaled[1], "core", perm=SWAP)
    partial = (scaled[0] + partner).astype(jnp.bfloat16)
    back = lax.all_to_all(partial, CHIPS, split_axis=0, concat_axis=0, tiled=True)
    mixed = jnp.sum(back.astype(jnp.float32), axis=0)
    return mixed.astype(jnp.bfloat16)


def solution(mesh):
    grp, blk = mesh.devices.shape
    ylo = 2
    fine = Mesh(
        mesh.devices.reshape(2, grp // 2, 4, blk // (4 * ylo), ylo),
        ("yhi", "core", "x", "z", "ylo"),
    )
    rows = P(("yhi", "core", "x", "z", "ylo"), None)
    weights = P(("yhi", "core"), ("x", "z", "ylo"), None)
    return jax.shard_map(
        per_device,
        mesh=fine,
        in_specs=(rows, rows, rows, weights, weights, weights),
        out_specs=rows,
        check_vma=False,
    )
```

```python
import jax
import jax.numpy as jnp
from jax import lax
from jax.sharding import Mesh
from jax.sharding import PartitionSpec as P

CHIPS = ("yhi", "ylo")
SWAP = [(0, 1), (1, 0)]


def ring_of_four(value, axis):
    ahead = [(i, (i + 1) % 4) for i in range(4)]
    behind = [(i, (i - 1) % 4) for i in range(4)]
    from_minus = lax.ppermute(value, axis, perm=ahead)
    from_plus = lax.ppermute(value, axis, perm=behind)
    half = value.shape[-1] // 2
    far = jnp.concatenate(
        [
            lax.ppermute(from_minus[..., :half], axis, perm=ahead),
            lax.ppermute(from_plus[..., half:], axis, perm=behind),
        ],
        axis=-1,
    )
    return jnp.stack([value, from_plus, far, from_minus])


def expert_weights(w_gate, w_up, w_down, ylo):
    stacked = jnp.stack([w_gate, w_up, w_down], axis=1)
    rows = stacked.shape[2]
    padded = -(-rows // 16) * 16
    stacked = jnp.pad(stacked, ((0, 0), (0, 0), (0, padded - rows), (0, 0)))
    keep = lax.dynamic_index_in_dim(stacked, ylo, axis=0, keepdims=False)
    send = lax.dynamic_index_in_dim(stacked, 1 - ylo, axis=0, keepdims=False)
    got = lax.ppermute(send, "ylo", perm=SWAP)
    first_a = ring_of_four(keep, "z")
    first_b = ring_of_four(got, "x")
    first_a, first_b = lax.optimization_barrier((first_a, first_b))
    gate_up_a = ring_of_four(first_a[:, :2], "x")
    gate_up_b = ring_of_four(first_b[:, :2], "z")
    gate_up_a, gate_up_b, down_a, down_b = lax.optimization_barrier(
        (gate_up_a, gate_up_b, first_a[:, 2], first_b[:, 2])
    )
    down_a = ring_of_four(down_a, "x")
    down_b = ring_of_four(down_b, "z")
    width = stacked.shape[-1]
    sets = []
    for gate_up, down in ((gate_up_a, down_a), (gate_up_b, down_b)):
        gate_up = jnp.moveaxis(gate_up, 2, 0).reshape(2, -1, width)
        sets.append((gate_up[0], gate_up[1], down.reshape(-1, width)))
    return sets


def spread(value, chips):
    sent = jnp.broadcast_to(value[None], (chips,) + value.shape)
    mine = lax.all_to_all(sent, CHIPS, split_axis=0, concat_axis=0, tiled=True)
    other = lax.ppermute(mine, "core", perm=SWAP)
    return mine, other


def per_device(tokens, expert_ids, gate_weights, w_gate, w_up, w_down):
    ylo = lax.axis_index("ylo")
    chips = lax.axis_size("yhi") * lax.axis_size("ylo")
    expert = (lax.axis_index("yhi") * lax.axis_size("core") + lax.axis_index("core")) * 2 + ylo
    token_count, model_width = tokens.shape

    sets = expert_weights(w_gate, w_up, w_down, ylo)

    experts = jnp.arange(lax.axis_size("core") * chips, dtype=jnp.int32)
    weight = jnp.sum(
        jnp.where(expert_ids[:, :, None] == experts, gate_weights[:, :, None], 0.0), axis=1
    )
    high = lax.reduce_precision(weight, exponent_bits=8, mantissa_bits=7)
    low = weight - high
    packed = jnp.concatenate([high, low], axis=1).astype(jnp.bfloat16).T
    extra = packed.shape[0]
    packed = jnp.pad(packed, ((0, 0), (0, model_width - token_count)))
    mine, other = spread(jnp.concatenate([tokens, packed]), chips)
    both = jnp.concatenate([mine, other])
    rows = both[:, :token_count].reshape(-1, model_width)
    halves = jnp.swapaxes(both[:, token_count:, :token_count], 1, 2).astype(jnp.float32)
    table = (halves[..., : extra // 2] + halves[..., extra // 2 :]).reshape(-1, extra // 2)
    scale = lax.dynamic_index_in_dim(table, expert, axis=1, keepdims=True)

    out = None
    for weights in sets:
        gate_part = jnp.dot(rows, weights[0].T, preferred_element_type=jnp.float32)
        up_part = jnp.dot(rows, weights[1].T, preferred_element_type=jnp.float32)
        hidden = (jax.nn.silu(gate_part) * up_part).astype(jnp.bfloat16)
        part = jnp.dot(hidden, weights[2], preferred_element_type=jnp.float32)
        out = part if out is None else out + part
    out = out.astype(jnp.bfloat16)
    scaled = (out.astype(jnp.float32) * scale).reshape(2, chips, token_count, model_width)

    partner = lax.ppermute(scaled[1], "core", perm=SWAP)
    partial = (scaled[0] + partner).astype(jnp.bfloat16)
    back = lax.all_to_all(partial, CHIPS, split_axis=0, concat_axis=0, tiled=True)
    mixed = jnp.sum(back.astype(jnp.float32), axis=0)
    return mixed.astype(jnp.bfloat16)


def solution(mesh):
    grp, blk = mesh.devices.shape
    ylo = 2
    fine = Mesh(
        mesh.devices.reshape(2, grp // 2, 4, blk // (4 * ylo), ylo),
        ("yhi", "core", "x", "z", "ylo"),
    )
    rows = P(("yhi", "core", "x", "z", "ylo"), None)
    weights = P(("yhi", "core"), ("x", "z", "ylo"), None)
    return jax.shard_map(
        per_device,
        mesh=fine,
        in_specs=(rows, rows, rows, weights, weights, weights),
        out_specs=rows,
        check_vma=False,
    )
```

```python
import jax
import jax.numpy as jnp
from jax import lax
from jax.sharding import Mesh
from jax.sharding import PartitionSpec as P

CHIPS = ("yhi", "ylo")
SWAP = [(0, 1), (1, 0)]


def ring_of_four(value, axis):
    ahead = [(i, (i + 1) % 4) for i in range(4)]
    behind = [(i, (i - 1) % 4) for i in range(4)]
    from_minus = lax.ppermute(value, axis, perm=ahead)
    from_plus = lax.ppermute(value, axis, perm=behind)
    half = value.shape[-1] // 2
    far = jnp.concatenate(
        [
            lax.ppermute(from_minus[..., :half], axis, perm=ahead),
            lax.ppermute(from_plus[..., half:], axis, perm=behind),
        ],
        axis=-1,
    )
    return jnp.stack([value, from_plus, far, from_minus])


def expert_weights(w_gate, w_up, w_down, ylo):
    stacked = jnp.stack([w_gate, w_up, w_down], axis=1)
    rows = stacked.shape[2]
    padded = -(-rows // 16) * 16
    stacked = jnp.pad(stacked, ((0, 0), (0, 0), (0, padded - rows), (0, 0)))
    keep = lax.dynamic_index_in_dim(stacked, ylo, axis=0, keepdims=False)
    send = lax.dynamic_index_in_dim(stacked, 1 - ylo, axis=0, keepdims=False)
    got = lax.ppermute(send, "ylo", perm=SWAP)
    first_a = ring_of_four(keep, "z")
    first_b = ring_of_four(got, "x")
    first_a, first_b = lax.optimization_barrier((first_a, first_b))
    gate_up_a = ring_of_four(first_a[:, :2], "x")
    gate_up_b = ring_of_four(first_b[:, :2], "z")
    gate_up_a, gate_up_b, down_a, down_b = lax.optimization_barrier(
        (gate_up_a, gate_up_b, first_a[:, 2], first_b[:, 2])
    )
    down_a = ring_of_four(down_a, "x")
    down_b = ring_of_four(down_b, "z")
    width = stacked.shape[-1]
    sets = []
    for gate_up, down in ((gate_up_a, down_a), (gate_up_b, down_b)):
        gate_up = jnp.moveaxis(gate_up, 2, 0).reshape(2, -1, width)
        sets.append((gate_up[0], gate_up[1], down.reshape(-1, width)))
    return sets


def spread(value, chips):
    sent = jnp.broadcast_to(value[None], (chips,) + value.shape)
    mine = lax.all_to_all(sent, CHIPS, split_axis=0, concat_axis=0, tiled=True)
    other = lax.ppermute(mine, "core", perm=SWAP)
    return mine, other


def per_device(tokens, expert_ids, gate_weights, w_gate, w_up, w_down):
    ylo = lax.axis_index("ylo")
    chips = lax.axis_size("yhi") * lax.axis_size("ylo")
    expert = (lax.axis_index("yhi") * lax.axis_size("core") + lax.axis_index("core")) * 2 + ylo
    token_count, model_width = tokens.shape

    sets = expert_weights(w_gate, w_up, w_down, ylo)

    experts = jnp.arange(lax.axis_size("core") * chips, dtype=jnp.int32)
    weight = jnp.sum(
        jnp.where(expert_ids[:, :, None] == experts, gate_weights[:, :, None], 0.0), axis=1
    )
    high = lax.reduce_precision(weight, exponent_bits=8, mantissa_bits=7)
    low = weight - high
    packed = jnp.concatenate([high, low], axis=1).astype(jnp.bfloat16).T
    extra = packed.shape[0]
    packed = jnp.pad(packed, ((0, 0), (0, model_width - token_count)))
    mine, other = spread(jnp.concatenate([tokens, packed]), chips)
    both = jnp.concatenate([mine, other])
    rows = both[:, :token_count].reshape(-1, model_width)
    halves = jnp.swapaxes(both[:, token_count:, :token_count], 1, 2).astype(jnp.float32)
    table = (halves[..., : extra // 2] + halves[..., extra // 2 :]).reshape(-1, extra // 2)
    scale = lax.dynamic_index_in_dim(table, expert, axis=1, keepdims=True)

    out = None
    for weights in sets:
        gate_part = jnp.dot(rows, weights[0].T, preferred_element_type=jnp.float32)
        up_part = jnp.dot(rows, weights[1].T, preferred_element_type=jnp.float32)
        hidden = (jax.nn.silu(gate_part) * up_part).astype(jnp.bfloat16)
        hidden = lax.optimization_barrier(hidden)
        part = jnp.dot(hidden, weights[2], preferred_element_type=jnp.float32)
        out = part if out is None else out + part
    out = out.astype(jnp.bfloat16)
    scaled = (out.astype(jnp.float32) * scale).reshape(2, chips, token_count, model_width)

    partner = lax.ppermute(scaled[1], "core", perm=SWAP)
    partial = (scaled[0] + partner).astype(jnp.bfloat16)
    back = lax.all_to_all(partial, CHIPS, split_axis=0, concat_axis=0, tiled=True)
    mixed = jnp.sum(back.astype(jnp.float32), axis=0)
    return mixed.astype(jnp.bfloat16)


def solution(mesh):
    grp, blk = mesh.devices.shape
    ylo = 2
    fine = Mesh(
        mesh.devices.reshape(2, grp // 2, 4, blk // (4 * ylo), ylo),
        ("yhi", "core", "x", "z", "ylo"),
    )
    rows = P(("yhi", "core", "x", "z", "ylo"), None)
    weights = P(("yhi", "core"), ("x", "z", "ylo"), None)
    return jax.shard_map(
        per_device,
        mesh=fine,
        in_specs=(rows, rows, rows, weights, weights, weights),
        out_specs=rows,
        check_vma=False,
    )
```

```python
import jax
import jax.numpy as jnp
from jax import lax
from jax.sharding import Mesh
from jax.sharding import PartitionSpec as P

CHIPS = ("yhi", "ylo")
SWAP = [(0, 1), (1, 0)]


def ring_of_four(value, axis):
    ahead = [(i, (i + 1) % 4) for i in range(4)]
    behind = [(i, (i - 1) % 4) for i in range(4)]
    from_minus = lax.ppermute(value, axis, perm=ahead)
    from_plus = lax.ppermute(value, axis, perm=behind)
    half = value.shape[-1] // 2
    far = jnp.concatenate(
        [
            lax.ppermute(from_minus[..., :half], axis, perm=ahead),
            lax.ppermute(from_plus[..., half:], axis, perm=behind),
        ],
        axis=-1,
    )
    return jnp.stack([value, from_plus, far, from_minus])


def expert_weights(w_gate, w_up, w_down, ylo):
    stacked = jnp.stack([w_gate, w_up, w_down], axis=1)
    rows = stacked.shape[2]
    padded = -(-rows // 16) * 16
    stacked = jnp.pad(stacked, ((0, 0), (0, 0), (0, padded - rows), (0, 0)))
    keep = lax.dynamic_index_in_dim(stacked, ylo, axis=0, keepdims=False)
    send = lax.dynamic_index_in_dim(stacked, 1 - ylo, axis=0, keepdims=False)
    got = lax.ppermute(send, "ylo", perm=SWAP)
    first_a = ring_of_four(keep, "z")
    first_b = ring_of_four(got, "x")
    first_a, first_b = lax.optimization_barrier((first_a, first_b))
    gate_up_a = ring_of_four(first_a[:, :2], "x")
    gate_up_b = ring_of_four(first_b[:, :2], "z")
    gate_up_a, gate_up_b, down_a, down_b = lax.optimization_barrier(
        (gate_up_a, gate_up_b, first_a[:, 2], first_b[:, 2])
    )
    down_a = ring_of_four(down_a, "x")
    down_b = ring_of_four(down_b, "z")
    width = stacked.shape[-1]
    sets = []
    for gate_up, down in ((gate_up_a, down_a), (gate_up_b, down_b)):
        gate_up = jnp.moveaxis(gate_up, 2, 0).reshape(2, -1, width)
        sets.append((gate_up[0], gate_up[1], down.reshape(-1, width)))
    return sets


def spread(value, chips):
    sent = jnp.broadcast_to(value[None], (chips,) + value.shape)
    mine = lax.all_to_all(sent, CHIPS, split_axis=0, concat_axis=0, tiled=True)
    other = lax.ppermute(mine, "core", perm=SWAP)
    return mine, other


def per_device(tokens, expert_ids, gate_weights, w_gate, w_up, w_down):
    ylo = lax.axis_index("ylo")
    chips = lax.axis_size("yhi") * lax.axis_size("ylo")
    expert = (lax.axis_index("yhi") * lax.axis_size("core") + lax.axis_index("core")) * 2 + ylo
    token_count, model_width = tokens.shape

    sets = expert_weights(w_gate, w_up, w_down, ylo)

    experts = jnp.arange(lax.axis_size("core") * chips, dtype=jnp.int32)
    weight = jnp.sum(
        jnp.where(expert_ids[:, :, None] == experts, gate_weights[:, :, None], 0.0), axis=1
    )
    high = lax.reduce_precision(weight, exponent_bits=8, mantissa_bits=7)
    low = weight - high
    packed = jnp.concatenate([high, low], axis=1).astype(jnp.bfloat16).T
    extra = packed.shape[0]
    packed = jnp.pad(packed, ((0, 0), (0, model_width - token_count)))
    mine, other = spread(jnp.concatenate([tokens, packed]), chips)
    both = jnp.concatenate([mine, other])
    rows = both[:, :token_count].reshape(-1, model_width)
    halves = jnp.swapaxes(both[:, token_count:, :token_count], 1, 2).astype(jnp.float32)
    table = (halves[..., : extra // 2] + halves[..., extra // 2 :]).reshape(-1, extra // 2)
    scale = lax.dynamic_index_in_dim(table, expert, axis=1, keepdims=True)

    hiddens = []
    for weights in sets:
        gate_part = jnp.dot(rows, weights[0].T, preferred_element_type=jnp.float32)
        up_part = jnp.dot(rows, weights[1].T, preferred_element_type=jnp.float32)
        hidden = (jax.nn.silu(gate_part) * up_part).astype(jnp.bfloat16)
        hiddens.append(lax.optimization_barrier(hidden))

    def down(hiddens, first, last):
        out = None
        for hidden, weights in zip(hiddens, sets):
            part = jnp.dot(hidden[first:last], weights[2], preferred_element_type=jnp.float32)
            out = part if out is None else out + part
        weighted = out.astype(jnp.bfloat16).astype(jnp.float32) * scale[first:last]
        return weighted.reshape(chips, token_count, model_width)

    half = chips * token_count
    theirs = down(hiddens, half, 2 * half)
    hiddens, theirs = lax.optimization_barrier((hiddens, theirs))
    partner = lax.ppermute(theirs, "core", perm=SWAP)
    partial = (down(hiddens, 0, half) + partner).astype(jnp.bfloat16)
    back = lax.all_to_all(partial, CHIPS, split_axis=0, concat_axis=0, tiled=True)
    mixed = jnp.sum(back.astype(jnp.float32), axis=0)
    return mixed.astype(jnp.bfloat16)


def solution(mesh):
    grp, blk = mesh.devices.shape
    ylo = 2
    fine = Mesh(
        mesh.devices.reshape(2, grp // 2, 4, blk // (4 * ylo), ylo),
        ("yhi", "core", "x", "z", "ylo"),
    )
    rows = P(("yhi", "core", "x", "z", "ylo"), None)
    weights = P(("yhi", "core"), ("x", "z", "ylo"), None)
    return jax.shard_map(
        per_device,
        mesh=fine,
        in_specs=(rows, rows, rows, weights, weights, weights),
        out_specs=rows,
        check_vma=False,
    )
```

```python
import jax
import jax.numpy as jnp
from jax import lax
from jax.sharding import Mesh
from jax.sharding import PartitionSpec as P

CHIPS = ("yhi", "ylo")
SWAP = [(0, 1), (1, 0)]


AHEAD = [(i, (i + 1) % 4) for i in range(4)]
BEHIND = [(i, (i - 1) % 4) for i in range(4)]


def first_hop(value, axis):
    return lax.ppermute(value, axis, perm=AHEAD), lax.ppermute(value, axis, perm=BEHIND)


def far_hop(value, near, axis):
    from_minus, from_plus = near
    half = value.shape[-1] // 2
    far = jnp.concatenate(
        [
            lax.ppermute(from_minus[..., :half], axis, perm=AHEAD),
            lax.ppermute(from_plus[..., half:], axis, perm=BEHIND),
        ],
        axis=-1,
    )
    return jnp.stack([value, from_plus, far, from_minus])


def ring_of_four(value, axis):
    return far_hop(value, first_hop(value, axis), axis)


def expert_weights(w_gate, w_up, w_down, ylo):
    stacked = jnp.stack([w_gate, w_up, w_down], axis=1)
    rows = stacked.shape[2]
    padded = -(-rows // 16) * 16
    stacked = jnp.pad(stacked, ((0, 0), (0, 0), (0, padded - rows), (0, 0)))
    keep = lax.dynamic_index_in_dim(stacked, ylo, axis=0, keepdims=False)
    send = lax.dynamic_index_in_dim(stacked, 1 - ylo, axis=0, keepdims=False)
    got = lax.ppermute(send, "ylo", perm=SWAP)
    first_a = ring_of_four(keep, "z")
    first_b = ring_of_four(got, "x")
    first_a, first_b = lax.optimization_barrier((first_a, first_b))
    gate_up_a = ring_of_four(first_a[:, :2], "x")
    gate_up_b = ring_of_four(first_b[:, :2], "z")
    gate_up_a, gate_up_b, down_a, down_b = lax.optimization_barrier(
        (gate_up_a, gate_up_b, first_a[:, 2], first_b[:, 2])
    )
    width = stacked.shape[-1]
    gate_ups = [jnp.moveaxis(g, 2, 0).reshape(2, -1, width) for g in (gate_up_a, gate_up_b)]
    return gate_ups, (down_a, first_hop(down_a, "x")), (down_b, first_hop(down_b, "z"))


def finish_down(pending_a, pending_b):
    width = pending_a[0].shape[-1]
    return [
        far_hop(*pending_a, "x").reshape(-1, width),
        far_hop(*pending_b, "z").reshape(-1, width),
    ]


def spread(value, chips):
    sent = jnp.broadcast_to(value[None], (chips,) + value.shape)
    mine = lax.all_to_all(sent, CHIPS, split_axis=0, concat_axis=0, tiled=True)
    other = lax.ppermute(mine, "core", perm=SWAP)
    return mine, other


def per_device(tokens, expert_ids, gate_weights, w_gate, w_up, w_down):
    ylo = lax.axis_index("ylo")
    chips = lax.axis_size("yhi") * lax.axis_size("ylo")
    expert = (lax.axis_index("yhi") * lax.axis_size("core") + lax.axis_index("core")) * 2 + ylo
    token_count, model_width = tokens.shape

    gate_ups, pending_a, pending_b = expert_weights(w_gate, w_up, w_down, ylo)

    experts = jnp.arange(lax.axis_size("core") * chips, dtype=jnp.int32)
    weight = jnp.sum(
        jnp.where(expert_ids[:, :, None] == experts, gate_weights[:, :, None], 0.0), axis=1
    )
    high = lax.reduce_precision(weight, exponent_bits=8, mantissa_bits=7)
    low = weight - high
    packed = jnp.concatenate([high, low], axis=1).astype(jnp.bfloat16).T
    extra = packed.shape[0]
    packed = jnp.pad(packed, ((0, 0), (0, model_width - token_count)))
    mine, other = spread(jnp.concatenate([tokens, packed]), chips)
    both = jnp.concatenate([mine, other])
    rows = both[:, :token_count].reshape(-1, model_width)
    halves = jnp.swapaxes(both[:, token_count:, :token_count], 1, 2).astype(jnp.float32)
    table = (halves[..., : extra // 2] + halves[..., extra // 2 :]).reshape(-1, extra // 2)
    scale = lax.dynamic_index_in_dim(table, expert, axis=1, keepdims=True)

    gate_parts = [
        jnp.dot(rows, g[0].T, preferred_element_type=jnp.float32) for g in gate_ups
    ]
    late_rows, pending_a, pending_b = lax.optimization_barrier((rows, pending_a, pending_b))
    sets = [(g[0], g[1], d) for g, d in zip(gate_ups, finish_down(pending_a, pending_b))]
    hiddens = []
    for gate_part, weights in zip(gate_parts, sets):
        up_part = jnp.dot(late_rows, weights[1].T, preferred_element_type=jnp.float32)
        hidden = (jax.nn.silu(gate_part) * up_part).astype(jnp.bfloat16)
        hiddens.append(lax.optimization_barrier(hidden))

    def down(hiddens, first, last):
        out = None
        for hidden, weights in zip(hiddens, sets):
            part = jnp.dot(hidden[first:last], weights[2], preferred_element_type=jnp.float32)
            out = part if out is None else out + part
        weighted = out.astype(jnp.bfloat16).astype(jnp.float32) * scale[first:last]
        return weighted.reshape(chips, token_count, model_width)

    half = chips * token_count
    theirs = down(hiddens, half, 2 * half)
    hiddens, theirs = lax.optimization_barrier((hiddens, theirs))
    partner = lax.ppermute(theirs, "core", perm=SWAP)
    partial = (down(hiddens, 0, half) + partner).astype(jnp.bfloat16)
    back = lax.all_to_all(partial, CHIPS, split_axis=0, concat_axis=0, tiled=True)
    mixed = jnp.sum(back.astype(jnp.float32), axis=0)
    return mixed.astype(jnp.bfloat16)


def solution(mesh):
    grp, blk = mesh.devices.shape
    ylo = 2
    fine = Mesh(
        mesh.devices.reshape(2, grp // 2, 4, blk // (4 * ylo), ylo),
        ("yhi", "core", "x", "z", "ylo"),
    )
    rows = P(("yhi", "core", "x", "z", "ylo"), None)
    weights = P(("yhi", "core"), ("x", "z", "ylo"), None)
    return jax.shard_map(
        per_device,
        mesh=fine,
        in_specs=(rows, rows, rows, weights, weights, weights),
        out_specs=rows,
        check_vma=False,
    )
```

```python
import jax
import jax.numpy as jnp
from jax import lax
from jax.sharding import Mesh
from jax.sharding import PartitionSpec as P

CHIPS = ("yhi", "ylo")
SWAP = [(0, 1), (1, 0)]


AHEAD = [(i, (i + 1) % 4) for i in range(4)]
BEHIND = [(i, (i - 1) % 4) for i in range(4)]


def first_hop(value, axis):
    return lax.ppermute(value, axis, perm=AHEAD), lax.ppermute(value, axis, perm=BEHIND)


def far_pieces(value, near, axis):
    from_minus, from_plus = near
    half = value.shape[-1] // 2
    far = jnp.concatenate(
        [
            lax.ppermute(from_minus[..., :half], axis, perm=AHEAD),
            lax.ppermute(from_plus[..., half:], axis, perm=BEHIND),
        ],
        axis=-1,
    )
    return (value, from_plus, far, from_minus)


def far_hop(value, near, axis):
    return jnp.stack(far_pieces(value, near, axis))


def ring_of_four(value, axis):
    return far_hop(value, first_hop(value, axis), axis)


def expert_weights(w_gate, w_up, w_down, ylo, early):
    stacked = jnp.stack([w_gate, w_up, w_down], axis=1)
    rows = stacked.shape[2]
    padded = -(-rows // 16) * 16
    stacked = jnp.pad(stacked, ((0, 0), (0, 0), (0, padded - rows), (0, 0)))
    keep = lax.dynamic_index_in_dim(stacked, ylo, axis=0, keepdims=False)
    send = lax.dynamic_index_in_dim(stacked, 1 - ylo, axis=0, keepdims=False)
    got = lax.ppermute(send, "ylo", perm=SWAP)
    first_a = ring_of_four(keep, "z")
    first_b = ring_of_four(got, "x")
    first_a, first_b, early = lax.optimization_barrier((first_a, first_b, early))
    lead_a, lead_b = first_a[:, :2], first_b[:, :2]
    gate_up_a = far_pieces(lead_a, first_hop(lead_a, "x"), "x")
    gate_up_b = far_pieces(lead_b, first_hop(lead_b, "z"), "z")
    gate_up_a, gate_up_b, down_a, down_b = lax.optimization_barrier(
        (gate_up_a, gate_up_b, first_a[:, 2], first_b[:, 2])
    )
    gate_up_a, gate_up_b = jnp.stack(gate_up_a), jnp.stack(gate_up_b)
    width = stacked.shape[-1]
    gate_ups = [jnp.moveaxis(g, 2, 0).reshape(2, -1, width) for g in (gate_up_a, gate_up_b)]
    return gate_ups, (down_a, first_hop(down_a, "x")), (down_b, first_hop(down_b, "z")), early


def finish_down(pending_a, pending_b):
    width = pending_a[0].shape[-1]
    return [
        far_hop(*pending_a, "x").reshape(-1, width),
        far_hop(*pending_b, "z").reshape(-1, width),
    ]


def spread_chips(value, chips):
    sent = jnp.broadcast_to(value[None], (chips,) + value.shape)
    return lax.all_to_all(sent, CHIPS, split_axis=0, concat_axis=0, tiled=True)


def per_device(tokens, expert_ids, gate_weights, w_gate, w_up, w_down):
    ylo = lax.axis_index("ylo")
    chips = lax.axis_size("yhi") * lax.axis_size("ylo")
    expert = (lax.axis_index("yhi") * lax.axis_size("core") + lax.axis_index("core")) * 2 + ylo
    token_count, model_width = tokens.shape


    experts = jnp.arange(lax.axis_size("core") * chips, dtype=jnp.int32)
    weight = jnp.sum(
        jnp.where(expert_ids[:, :, None] == experts, gate_weights[:, :, None], 0.0), axis=1
    )
    high = lax.reduce_precision(weight, exponent_bits=8, mantissa_bits=7)
    low = weight - high
    packed = jnp.concatenate([high, low], axis=1).astype(jnp.bfloat16).T
    extra = packed.shape[0]
    packed = jnp.pad(packed, ((0, 0), (0, model_width - token_count)))
    mine = spread_chips(jnp.concatenate([tokens, packed]), chips)
    gate_ups, pending_a, pending_b, mine = expert_weights(w_gate, w_up, w_down, ylo, mine)
    other = lax.ppermute(mine, "core", perm=SWAP)
    both = jnp.concatenate([mine, other])
    rows = both[:, :token_count].reshape(-1, model_width)
    halves = jnp.swapaxes(both[:, token_count:, :token_count], 1, 2).astype(jnp.float32)
    table = (halves[..., : extra // 2] + halves[..., extra // 2 :]).reshape(-1, extra // 2)
    scale = lax.dynamic_index_in_dim(table, expert, axis=1, keepdims=True)

    gate_parts = [
        jnp.dot(rows, g[0].T, preferred_element_type=jnp.float32) for g in gate_ups
    ]
    late_rows, pending_a, pending_b = lax.optimization_barrier((rows, pending_a, pending_b))
    sets = [(g[0], g[1], d) for g, d in zip(gate_ups, finish_down(pending_a, pending_b))]
    hiddens = []
    for gate_part, weights in zip(gate_parts, sets):
        up_part = jnp.dot(late_rows, weights[1].T, preferred_element_type=jnp.float32)
        hidden = (jax.nn.silu(gate_part) * up_part).astype(jnp.bfloat16)
        hiddens.append(lax.optimization_barrier(hidden))

    def down(hiddens, first, last):
        out = None
        for hidden, weights in zip(hiddens, sets):
            part = jnp.dot(hidden[first:last], weights[2], preferred_element_type=jnp.float32)
            out = part if out is None else out + part
        weighted = out.astype(jnp.bfloat16).astype(jnp.float32) * scale[first:last]
        return weighted.reshape(chips, token_count, model_width)

    half = chips * token_count
    theirs = down(hiddens, half, 2 * half)
    hiddens, theirs = lax.optimization_barrier((hiddens, theirs))
    partner = lax.ppermute(theirs, "core", perm=SWAP)
    partial = (down(hiddens, 0, half) + partner).astype(jnp.bfloat16)
    back = lax.all_to_all(partial, CHIPS, split_axis=0, concat_axis=0, tiled=True)
    mixed = jnp.sum(back.astype(jnp.float32), axis=0)
    return mixed.astype(jnp.bfloat16)


def solution(mesh):
    grp, blk = mesh.devices.shape
    ylo = 2
    fine = Mesh(
        mesh.devices.reshape(2, grp // 2, 4, blk // (4 * ylo), ylo),
        ("yhi", "core", "x", "z", "ylo"),
    )
    rows = P(("yhi", "core", "x", "z", "ylo"), None)
    weights = P(("yhi", "core"), ("x", "z", "ylo"), None)
    return jax.shard_map(
        per_device,
        mesh=fine,
        in_specs=(rows, rows, rows, weights, weights, weights),
        out_specs=rows,
        check_vma=False,
    )
```

```python
import jax
import jax.numpy as jnp
from jax import lax
from jax.sharding import Mesh
from jax.sharding import PartitionSpec as P

CHIPS = ("yhi", "ylo")
SWAP = [(0, 1), (1, 0)]


AHEAD = [(i, (i + 1) % 4) for i in range(4)]
BEHIND = [(i, (i - 1) % 4) for i in range(4)]


def first_hop(value, axis):
    return lax.ppermute(value, axis, perm=AHEAD), lax.ppermute(value, axis, perm=BEHIND)


def far_hop(value, near, axis):
    from_minus, from_plus = near
    half = value.shape[-1] // 2
    far = jnp.concatenate(
        [
            lax.ppermute(from_minus[..., :half], axis, perm=AHEAD),
            lax.ppermute(from_plus[..., half:], axis, perm=BEHIND),
        ],
        axis=-1,
    )
    return jnp.stack([value, from_plus, far, from_minus])


def ring_of_four(value, axis):
    return far_hop(value, first_hop(value, axis), axis)


def expert_weights(w_gate, w_up, w_down, ylo):
    stacked = jnp.stack([w_gate, w_up, w_down], axis=1)
    rows = stacked.shape[2]
    padded = -(-rows // 16) * 16
    stacked = jnp.pad(stacked, ((0, 0), (0, 0), (0, padded - rows), (0, 0)))
    keep = lax.dynamic_index_in_dim(stacked, ylo, axis=0, keepdims=False)
    send = lax.dynamic_index_in_dim(stacked, 1 - ylo, axis=0, keepdims=False)
    got = lax.ppermute(send, "ylo", perm=SWAP)
    down_a = lax.all_gather(keep[2], ("x", "z"), axis=0, tiled=False)
    down_b = lax.all_gather(got[2], ("x", "z"), axis=0, tiled=False)
    first_a = ring_of_four(keep[:2], "z")
    first_b = ring_of_four(got[:2], "x")
    first_a, first_b = lax.optimization_barrier((first_a, first_b))
    gate_up_a = ring_of_four(first_a, "x")
    gate_up_b = ring_of_four(first_b, "z")
    width = stacked.shape[-1]
    x, z = lax.axis_index("x"), lax.axis_index("z")
    sets = []
    for gate_up, down, z_first in ((gate_up_a, down_a, True), (gate_up_b, down_b, False)):
        gate_up = jnp.moveaxis(gate_up, 2, 0).reshape(2, -1, width)
        down = down.reshape((4, 4) + down.shape[1:])
        down = jnp.roll(jnp.roll(down, -x, axis=0), -z, axis=1)
        if not z_first:
            down = jnp.swapaxes(down, 0, 1)
        sets.append((gate_up[0], gate_up[1], down.reshape(-1, width)))
    return sets


def spread(value, chips):
    sent = jnp.broadcast_to(value[None], (chips,) + value.shape)
    mine = lax.all_to_all(sent, CHIPS, split_axis=0, concat_axis=0, tiled=True)
    other = lax.ppermute(mine, "core", perm=SWAP)
    return mine, other


def per_device(tokens, expert_ids, gate_weights, w_gate, w_up, w_down):
    ylo = lax.axis_index("ylo")
    chips = lax.axis_size("yhi") * lax.axis_size("ylo")
    expert = (lax.axis_index("yhi") * lax.axis_size("core") + lax.axis_index("core")) * 2 + ylo
    token_count, model_width = tokens.shape

    sets = expert_weights(w_gate, w_up, w_down, ylo)

    experts = jnp.arange(lax.axis_size("core") * chips, dtype=jnp.int32)
    weight = jnp.sum(
        jnp.where(expert_ids[:, :, None] == experts, gate_weights[:, :, None], 0.0), axis=1
    )
    high = lax.reduce_precision(weight, exponent_bits=8, mantissa_bits=7)
    low = weight - high
    packed = jnp.concatenate([high, low], axis=1).astype(jnp.bfloat16).T
    extra = packed.shape[0]
    packed = jnp.pad(packed, ((0, 0), (0, model_width - token_count)))
    mine, other = spread(jnp.concatenate([tokens, packed]), chips)
    both = jnp.concatenate([mine, other])
    rows = both[:, :token_count].reshape(-1, model_width)
    halves = jnp.swapaxes(both[:, token_count:, :token_count], 1, 2).astype(jnp.float32)
    table = (halves[..., : extra // 2] + halves[..., extra // 2 :]).reshape(-1, extra // 2)
    scale = lax.dynamic_index_in_dim(table, expert, axis=1, keepdims=True)

    hiddens = []
    for weights in sets:
        gate_part = jnp.dot(rows, weights[0].T, preferred_element_type=jnp.float32)
        up_part = jnp.dot(rows, weights[1].T, preferred_element_type=jnp.float32)
        hidden = (jax.nn.silu(gate_part) * up_part).astype(jnp.bfloat16)
        hiddens.append(lax.optimization_barrier(hidden))

    def down(hiddens, first, last):
        out = None
        for hidden, weights in zip(hiddens, sets):
            part = jnp.dot(hidden[first:last], weights[2], preferred_element_type=jnp.float32)
            out = part if out is None else out + part
        weighted = out.astype(jnp.bfloat16).astype(jnp.float32) * scale[first:last]
        return weighted.reshape(chips, token_count, model_width)

    half = chips * token_count
    theirs = down(hiddens, half, 2 * half)
    hiddens, theirs = lax.optimization_barrier((hiddens, theirs))
    partner = lax.ppermute(theirs, "core", perm=SWAP)
    partial = (down(hiddens, 0, half) + partner).astype(jnp.bfloat16)
    back = lax.all_to_all(partial, CHIPS, split_axis=0, concat_axis=0, tiled=True)
    mixed = jnp.sum(back.astype(jnp.float32), axis=0)
    return mixed.astype(jnp.bfloat16)


def solution(mesh):
    grp, blk = mesh.devices.shape
    ylo = 2
    fine = Mesh(
        mesh.devices.reshape(2, grp // 2, 4, blk // (4 * ylo), ylo),
        ("yhi", "core", "x", "z", "ylo"),
    )
    rows = P(("yhi", "core", "x", "z", "ylo"), None)
    weights = P(("yhi", "core"), ("x", "z", "ylo"), None)
    return jax.shard_map(
        per_device,
        mesh=fine,
        in_specs=(rows, rows, rows, weights, weights, weights),
        out_specs=rows,
        check_vma=False,
    )
```

```python
import jax
import jax.numpy as jnp
from jax import lax
from jax.sharding import Mesh
from jax.sharding import PartitionSpec as P

CHIPS = ("yhi", "ylo")
SWAP = [(0, 1), (1, 0)]


AHEAD = [(i, (i + 1) % 4) for i in range(4)]
BEHIND = [(i, (i - 1) % 4) for i in range(4)]


def first_hop(value, axis):
    return lax.ppermute(value, axis, perm=AHEAD), lax.ppermute(value, axis, perm=BEHIND)


def far_hop(value, near, axis):
    from_minus, from_plus = near
    half = value.shape[-1] // 2
    far = jnp.concatenate(
        [
            lax.ppermute(from_minus[..., :half], axis, perm=AHEAD),
            lax.ppermute(from_plus[..., half:], axis, perm=BEHIND),
        ],
        axis=-1,
    )
    return jnp.stack([value, from_plus, far, from_minus])


def ring_of_four(value, axis):
    return far_hop(value, first_hop(value, axis), axis)


def expert_weights(w_gate, w_up, w_down, ylo):
    stacked = jnp.stack([w_gate, w_up, w_down], axis=1)
    rows = stacked.shape[2]
    padded = -(-rows // 16) * 16
    stacked = jnp.pad(stacked, ((0, 0), (0, 0), (0, padded - rows), (0, 0)))
    keep = lax.dynamic_index_in_dim(stacked, ylo, axis=0, keepdims=False)
    send = lax.dynamic_index_in_dim(stacked, 1 - ylo, axis=0, keepdims=False)
    got = lax.ppermute(send, "ylo", perm=SWAP)
    first_a = ring_of_four(keep, "z")
    first_b = ring_of_four(got, "x")
    first_a, first_b = lax.optimization_barrier((first_a, first_b))
    gate_up_a = ring_of_four(first_a[:, :2], "x")
    gate_up_b = ring_of_four(first_b[:, :2], "z")
    gate_up_a, gate_up_b, down_a, down_b = lax.optimization_barrier(
        (gate_up_a, gate_up_b, first_a[:, 2], first_b[:, 2])
    )
    width = stacked.shape[-1]
    gate_ups = [jnp.moveaxis(g, 2, 0).reshape(2, -1, width) for g in (gate_up_a, gate_up_b)]
    return gate_ups, (down_a, first_hop(down_a, "x")), (down_b, first_hop(down_b, "z"))


def finish_down(pending_a, pending_b):
    width = pending_a[0].shape[-1]
    return [
        far_hop(*pending_a, "x").reshape(-1, width),
        far_hop(*pending_b, "z").reshape(-1, width),
    ]


def spread(value, chips):
    sent = jnp.broadcast_to(value[None], (chips,) + value.shape)
    mine = lax.all_to_all(sent, CHIPS, split_axis=0, concat_axis=0, tiled=True)
    other = lax.ppermute(mine, "core", perm=SWAP)
    return mine, other


def per_device(tokens, expert_ids, gate_weights, w_gate, w_up, w_down):
    ylo = lax.axis_index("ylo")
    chips = lax.axis_size("yhi") * lax.axis_size("ylo")
    expert = (lax.axis_index("yhi") * lax.axis_size("core") + lax.axis_index("core")) * 2 + ylo
    token_count, model_width = tokens.shape

    gate_ups, pending_a, pending_b = expert_weights(w_gate, w_up, w_down, ylo)

    experts = jnp.arange(lax.axis_size("core") * chips, dtype=jnp.int32)
    weight = jnp.sum(
        jnp.where(expert_ids[:, :, None] == experts, gate_weights[:, :, None], 0.0), axis=1
    )
    high = lax.reduce_precision(weight, exponent_bits=8, mantissa_bits=7)
    low = weight - high
    packed = jnp.concatenate([high, low], axis=1).astype(jnp.bfloat16).T
    extra = packed.shape[0]
    packed = jnp.pad(packed, ((0, 0), (0, model_width - token_count)))
    mine, other = spread(jnp.concatenate([tokens, packed]), chips)
    both = jnp.concatenate([mine, other])
    rows = both[:, :token_count].reshape(-1, model_width)
    halves = jnp.swapaxes(both[:, token_count:, :token_count], 1, 2).astype(jnp.float32)
    table = (halves[..., : extra // 2] + halves[..., extra // 2 :]).reshape(-1, extra // 2)
    scale = lax.dynamic_index_in_dim(table, expert, axis=1, keepdims=True)

    gate_parts = [
        jnp.dot(rows, g[0].T, preferred_element_type=jnp.float32) for g in gate_ups
    ]
    late_rows, pending_a, pending_b = lax.optimization_barrier((rows, pending_a, pending_b))
    sets = [(g[0], g[1], d) for g, d in zip(gate_ups, finish_down(pending_a, pending_b))]
    hiddens = []
    for gate_part, weights in zip(gate_parts, sets):
        up_part = jnp.dot(late_rows, weights[1].T, preferred_element_type=jnp.float32)
        hidden = (jax.nn.silu(gate_part) * up_part).astype(jnp.bfloat16)
        hiddens.append(lax.optimization_barrier(hidden))

    def down(hiddens, first, last):
        out = None
        for hidden, weights in zip(hiddens, sets):
            part = jnp.dot(hidden[first:last], weights[2], preferred_element_type=jnp.float32)
            out = part if out is None else out + part
        weighted = out.astype(jnp.bfloat16).astype(jnp.float32) * scale[first:last]
        return weighted.reshape(chips, token_count, model_width)

    half = chips * token_count
    theirs = down(hiddens, half, 2 * half)
    hiddens, theirs = lax.optimization_barrier((hiddens, theirs))
    partner = lax.ppermute(theirs, "core", perm=SWAP)
    partial = (down(hiddens, 0, half) + partner).astype(jnp.bfloat16)
    chip = lax.axis_index("yhi") * lax.axis_size("ylo") + ylo
    mixed = lax.dynamic_index_in_dim(partial, chip, keepdims=False).astype(jnp.float32)
    for offset in range(1, chips):
        piece = lax.dynamic_index_in_dim(partial, (chip + offset) % chips, keepdims=False)
        ring = [(i, (i + offset) % chips) for i in range(chips)]
        mixed = mixed + lax.ppermute(piece, CHIPS, perm=ring).astype(jnp.float32)
    return mixed.astype(jnp.bfloat16)


def solution(mesh):
    grp, blk = mesh.devices.shape
    ylo = 2
    fine = Mesh(
        mesh.devices.reshape(2, grp // 2, 4, blk // (4 * ylo), ylo),
        ("yhi", "core", "x", "z", "ylo"),
    )
    rows = P(("yhi", "core", "x", "z", "ylo"), None)
    weights = P(("yhi", "core"), ("x", "z", "ylo"), None)
    return jax.shard_map(
        per_device,
        mesh=fine,
        in_specs=(rows, rows, rows, weights, weights, weights),
        out_specs=rows,
        check_vma=False,
    )
```

```python
import jax
import jax.numpy as jnp
from jax import lax
from jax.sharding import Mesh
from jax.sharding import PartitionSpec as P

CHIPS = ("yhi", "ylo")
SWAP = [(0, 1), (1, 0)]


AHEAD = [(i, (i + 1) % 4) for i in range(4)]
BEHIND = [(i, (i - 1) % 4) for i in range(4)]


def first_hop(value, axis):
    return lax.ppermute(value, axis, perm=AHEAD), lax.ppermute(value, axis, perm=BEHIND)


def far_hop(value, near, axis):
    from_minus, from_plus = near
    split = 0 if value.shape[0] % 2 == 0 else value.ndim - 1
    half = value.shape[split] // 2
    far = jnp.concatenate(
        [
            lax.ppermute(lax.slice_in_dim(from_minus, 0, half, axis=split), axis, perm=AHEAD),
            lax.ppermute(
                lax.slice_in_dim(from_plus, half, 2 * half, axis=split), axis, perm=BEHIND
            ),
        ],
        axis=split,
    )
    return jnp.stack([value, from_plus, far, from_minus])


def ring_of_four(value, axis):
    return far_hop(value, first_hop(value, axis), axis)


def expert_weights(w_gate, w_up, w_down, ylo):
    stacked = jnp.stack([w_gate, w_up, w_down], axis=1)
    rows = stacked.shape[2]
    padded = -(-rows // 16) * 16
    stacked = jnp.pad(stacked, ((0, 0), (0, 0), (0, padded - rows), (0, 0)))
    keep = lax.dynamic_index_in_dim(stacked, ylo, axis=0, keepdims=False)
    send = lax.dynamic_index_in_dim(stacked, 1 - ylo, axis=0, keepdims=False)
    got = lax.ppermute(send, "ylo", perm=SWAP)
    first_a = ring_of_four(keep, "z")
    first_b = ring_of_four(got, "x")
    first_a, first_b = lax.optimization_barrier((first_a, first_b))
    gate_up_a = ring_of_four(first_a[:, :2], "x")
    gate_up_b = ring_of_four(first_b[:, :2], "z")
    gate_up_a, gate_up_b, down_a, down_b = lax.optimization_barrier(
        (gate_up_a, gate_up_b, first_a[:, 2], first_b[:, 2])
    )
    width = stacked.shape[-1]
    gate_ups = [jnp.moveaxis(g, 2, 0).reshape(2, -1, width) for g in (gate_up_a, gate_up_b)]
    return gate_ups, (down_a, first_hop(down_a, "x")), (down_b, first_hop(down_b, "z"))


def finish_down(pending_a, pending_b):
    width = pending_a[0].shape[-1]
    return [
        far_hop(*pending_a, "x").reshape(-1, width),
        far_hop(*pending_b, "z").reshape(-1, width),
    ]


def spread(value, chips):
    sent = jnp.broadcast_to(value[None], (chips,) + value.shape)
    mine = lax.all_to_all(sent, CHIPS, split_axis=0, concat_axis=0, tiled=True)
    other = lax.ppermute(mine, "core", perm=SWAP)
    return mine, other


def per_device(tokens, expert_ids, gate_weights, w_gate, w_up, w_down):
    ylo = lax.axis_index("ylo")
    chips = lax.axis_size("yhi") * lax.axis_size("ylo")
    expert = (lax.axis_index("yhi") * lax.axis_size("core") + lax.axis_index("core")) * 2 + ylo
    token_count, model_width = tokens.shape

    gate_ups, pending_a, pending_b = expert_weights(w_gate, w_up, w_down, ylo)

    experts = jnp.arange(lax.axis_size("core") * chips, dtype=jnp.int32)
    weight = jnp.sum(
        jnp.where(expert_ids[:, :, None] == experts, gate_weights[:, :, None], 0.0), axis=1
    )
    high = lax.reduce_precision(weight, exponent_bits=8, mantissa_bits=7)
    low = weight - high
    packed = jnp.concatenate([high, low], axis=1).astype(jnp.bfloat16).T
    extra = packed.shape[0]
    packed = jnp.pad(packed, ((0, 0), (0, model_width - token_count)))
    mine, other = spread(jnp.concatenate([tokens, packed]), chips)
    both = jnp.concatenate([mine, other])
    rows = both[:, :token_count].reshape(-1, model_width)
    halves = jnp.swapaxes(both[:, token_count:, :token_count], 1, 2).astype(jnp.float32)
    table = (halves[..., : extra // 2] + halves[..., extra // 2 :]).reshape(-1, extra // 2)
    scale = lax.dynamic_index_in_dim(table, expert, axis=1, keepdims=True)

    gate_parts = [
        jnp.dot(rows, g[0].T, preferred_element_type=jnp.float32) for g in gate_ups
    ]
    late_rows, pending_a, pending_b = lax.optimization_barrier((rows, pending_a, pending_b))
    sets = [(g[0], g[1], d) for g, d in zip(gate_ups, finish_down(pending_a, pending_b))]
    hiddens = []
    for gate_part, weights in zip(gate_parts, sets):
        up_part = jnp.dot(late_rows, weights[1].T, preferred_element_type=jnp.float32)
        hidden = (jax.nn.silu(gate_part) * up_part).astype(jnp.bfloat16)
        hiddens.append(lax.optimization_barrier(hidden))

    def down(hiddens, first, last):
        out = None
        for hidden, weights in zip(hiddens, sets):
            part = jnp.dot(hidden[first:last], weights[2], preferred_element_type=jnp.float32)
            out = part if out is None else out + part
        weighted = out.astype(jnp.bfloat16).astype(jnp.float32) * scale[first:last]
        return weighted.reshape(chips, token_count, model_width)

    half = chips * token_count
    theirs = down(hiddens, half, 2 * half)
    hiddens, theirs = lax.optimization_barrier((hiddens, theirs))
    partner = lax.ppermute(theirs, "core", perm=SWAP)
    partial = (down(hiddens, 0, half) + partner).astype(jnp.bfloat16)
    back = lax.all_to_all(partial, CHIPS, split_axis=0, concat_axis=0, tiled=True)
    mixed = jnp.sum(back.astype(jnp.float32), axis=0)
    return mixed.astype(jnp.bfloat16)


def solution(mesh):
    grp, blk = mesh.devices.shape
    ylo = 2
    fine = Mesh(
        mesh.devices.reshape(2, grp // 2, 4, blk // (4 * ylo), ylo),
        ("yhi", "core", "x", "z", "ylo"),
    )
    rows = P(("yhi", "core", "x", "z", "ylo"), None)
    weights = P(("yhi", "core"), ("x", "z", "ylo"), None)
    return jax.shard_map(
        per_device,
        mesh=fine,
        in_specs=(rows, rows, rows, weights, weights, weights),
        out_specs=rows,
        check_vma=False,
    )
```

```python
import jax
import jax.numpy as jnp
from jax import lax
from jax.sharding import Mesh
from jax.sharding import PartitionSpec as P

CHIPS = ("yhi", "ylo")
SWAP = [(0, 1), (1, 0)]


AHEAD = [(i, (i + 1) % 4) for i in range(4)]
BEHIND = [(i, (i - 1) % 4) for i in range(4)]


def first_hop(value, axis):
    return lax.ppermute(value, axis, perm=AHEAD), lax.ppermute(value, axis, perm=BEHIND)


def far_hop(value, near, axis):
    from_minus, from_plus = near
    half = value.shape[-1] // 2
    far = jnp.concatenate(
        [
            lax.ppermute(from_minus[..., :half], axis, perm=AHEAD),
            lax.ppermute(from_plus[..., half:], axis, perm=BEHIND),
        ],
        axis=-1,
    )
    return jnp.stack([value, from_plus, far, from_minus])


def ring_of_four(value, axis):
    return far_hop(value, first_hop(value, axis), axis)


def expert_weights(w_gate, w_up, w_down, ylo):
    stacked = jnp.stack([w_gate, w_up, w_down], axis=1)
    rows = stacked.shape[2]
    padded = -(-rows // 16) * 16
    stacked = jnp.pad(stacked, ((0, 0), (0, 0), (0, padded - rows), (0, 0)))
    keep = lax.dynamic_index_in_dim(stacked, ylo, axis=0, keepdims=False)
    send = lax.dynamic_index_in_dim(stacked, 1 - ylo, axis=0, keepdims=False)
    got = lax.ppermute(send, "ylo", perm=SWAP)
    first_a = ring_of_four(keep, "z")
    first_b = ring_of_four(got, "x")
    first_a, first_b = lax.optimization_barrier((first_a, first_b))
    gate_up_a = ring_of_four(first_a[:, :2], "x")
    gate_up_b = ring_of_four(first_b[:, :2], "z")
    gate_up_a, gate_up_b, down_a, down_b = lax.optimization_barrier(
        (gate_up_a, gate_up_b, first_a[:, 2], first_b[:, 2])
    )
    width = stacked.shape[-1]
    gate_ups = [jnp.moveaxis(g, 2, 0).reshape(2, -1, width) for g in (gate_up_a, gate_up_b)]
    return gate_ups, (down_a, first_hop(down_a, "x")), (down_b, first_hop(down_b, "z"))


def finish_down(pending_a, pending_b):
    width = pending_a[0].shape[-1]
    return [
        far_hop(*pending_a, "x").reshape(-1, width),
        far_hop(*pending_b, "z").reshape(-1, width),
    ]


def spread(value, chips):
    sent = jnp.broadcast_to(value[None], (chips,) + value.shape)
    mine = lax.all_to_all(sent, CHIPS, split_axis=0, concat_axis=0, tiled=True)
    other = lax.ppermute(mine, "core", perm=SWAP)
    return mine, other


def per_device(tokens, expert_ids, gate_weights, w_gate, w_up, w_down):
    ylo = lax.axis_index("ylo")
    chips = lax.axis_size("yhi") * lax.axis_size("ylo")
    expert = (lax.axis_index("yhi") * lax.axis_size("core") + lax.axis_index("core")) * 2 + ylo
    token_count, model_width = tokens.shape

    gate_ups, pending_a, pending_b = expert_weights(w_gate, w_up, w_down, ylo)

    experts = jnp.arange(lax.axis_size("core") * chips, dtype=jnp.int32)
    weight = jnp.sum(
        jnp.where(expert_ids[:, :, None] == experts, gate_weights[:, :, None], 0.0), axis=1
    )
    high = lax.reduce_precision(weight, exponent_bits=8, mantissa_bits=7)
    low = weight - high
    packed = jnp.concatenate([high, low], axis=1).astype(jnp.bfloat16).T
    extra = packed.shape[0]
    packed = jnp.pad(packed, ((0, 0), (0, model_width - token_count)))
    mine, other = spread(jnp.concatenate([tokens, packed]), chips)
    both = jnp.concatenate([mine, other])
    rows = both[:, :token_count].reshape(-1, model_width)
    halves = jnp.swapaxes(both[:, token_count:, :token_count], 1, 2).astype(jnp.float32)
    table = (halves[..., : extra // 2] + halves[..., extra // 2 :]).reshape(-1, extra // 2)
    scale = lax.dynamic_index_in_dim(table, expert, axis=1, keepdims=True)

    gate_parts = [
        jnp.dot(rows, g[0].T, preferred_element_type=jnp.float32) for g in gate_ups
    ]
    late_rows, pending_a, pending_b = lax.optimization_barrier((rows, pending_a, pending_b))
    sets = [(g[0], g[1], d) for g, d in zip(gate_ups, finish_down(pending_a, pending_b))]
    hiddens = []
    for gate_part, weights in zip(gate_parts, sets):
        up_part = jnp.dot(late_rows, weights[1].T, preferred_element_type=jnp.float32)
        hidden = (jax.nn.silu(gate_part) * up_part).astype(jnp.bfloat16)
        hiddens.append(lax.optimization_barrier(hidden))

    def down(hiddens, first, last):
        out = None
        for hidden, weights in zip(hiddens, sets):
            part = jnp.dot(hidden[first:last], weights[2], preferred_element_type=jnp.float32)
            out = part if out is None else out + part
        weighted = out.astype(jnp.bfloat16).astype(jnp.float32) * scale[first:last]
        return weighted.reshape(chips, token_count, model_width)

    half = chips * token_count
    theirs = down(hiddens, half, 2 * half)
    hiddens, theirs = lax.optimization_barrier((hiddens, theirs))
    partner = lax.ppermute(theirs.astype(jnp.bfloat16), "core", perm=SWAP)
    partial = (down(hiddens, 0, half) + partner.astype(jnp.float32)).astype(jnp.bfloat16)
    back = lax.all_to_all(partial, CHIPS, split_axis=0, concat_axis=0, tiled=True)
    mixed = jnp.sum(back.astype(jnp.float32), axis=0)
    return mixed.astype(jnp.bfloat16)


def solution(mesh):
    grp, blk = mesh.devices.shape
    ylo = 2
    fine = Mesh(
        mesh.devices.reshape(2, grp // 2, 4, blk // (4 * ylo), ylo),
        ("yhi", "core", "x", "z", "ylo"),
    )
    rows = P(("yhi", "core", "x", "z", "ylo"), None)
    weights = P(("yhi", "core"), ("x", "z", "ylo"), None)
    return jax.shard_map(
        per_device,
        mesh=fine,
        in_specs=(rows, rows, rows, weights, weights, weights),
        out_specs=rows,
        check_vma=False,
    )
```

```python
import jax
import jax.numpy as jnp
from jax import lax
from jax.sharding import Mesh
from jax.sharding import PartitionSpec as P

CHIPS = ("yhi", "ylo")
SWAP = [(0, 1), (1, 0)]


AHEAD = [(i, (i + 1) % 4) for i in range(4)]
BEHIND = [(i, (i - 1) % 4) for i in range(4)]


def first_hop(value, axis):
    return lax.ppermute(value, axis, perm=AHEAD), lax.ppermute(value, axis, perm=BEHIND)


def far_hop(value, near, axis):
    from_minus, from_plus = near
    half = value.shape[-1] // 2
    far = jnp.concatenate(
        [
            lax.ppermute(from_minus[..., :half], axis, perm=AHEAD),
            lax.ppermute(from_plus[..., half:], axis, perm=BEHIND),
        ],
        axis=-1,
    )
    return jnp.stack([value, from_plus, far, from_minus])


def ring_of_four(value, axis):
    return far_hop(value, first_hop(value, axis), axis)


def expert_weights(w_gate, w_up, w_down, ylo):
    stacked = jnp.stack([w_gate, w_up, w_down], axis=1)
    rows = stacked.shape[2]
    padded = -(-rows // 16) * 16
    stacked = jnp.pad(stacked, ((0, 0), (0, 0), (0, padded - rows), (0, 0)))
    keep = lax.dynamic_index_in_dim(stacked, ylo, axis=0, keepdims=False)
    send = lax.dynamic_index_in_dim(stacked, 1 - ylo, axis=0, keepdims=False)
    got = lax.ppermute(send, "ylo", perm=SWAP)
    first_a = ring_of_four(keep, "z")
    first_b = ring_of_four(got, "x")
    first_a, first_b = lax.optimization_barrier((first_a, first_b))
    lead_a, lead_b = first_a[:, :2], first_b[:, :2]
    near_a, near_b = first_hop(lead_a, "x"), first_hop(lead_b, "z")
    near_a, near_b, down_a, down_b = lax.optimization_barrier(
        (near_a, near_b, first_a[:, 2], first_b[:, 2])
    )
    gate_up_a = far_hop(lead_a, near_a, "x")
    gate_up_b = far_hop(lead_b, near_b, "z")
    width = stacked.shape[-1]
    gate_ups = [jnp.moveaxis(g, 2, 0).reshape(2, -1, width) for g in (gate_up_a, gate_up_b)]
    return gate_ups, (down_a, first_hop(down_a, "x")), (down_b, first_hop(down_b, "z"))


def finish_down(pending_a, pending_b):
    width = pending_a[0].shape[-1]
    return [
        far_hop(*pending_a, "x").reshape(-1, width),
        far_hop(*pending_b, "z").reshape(-1, width),
    ]


def spread(value, chips):
    sent = jnp.broadcast_to(value[None], (chips,) + value.shape)
    mine = lax.all_to_all(sent, CHIPS, split_axis=0, concat_axis=0, tiled=True)
    other = lax.ppermute(mine, "core", perm=SWAP)
    return mine, other


def per_device(tokens, expert_ids, gate_weights, w_gate, w_up, w_down):
    ylo = lax.axis_index("ylo")
    chips = lax.axis_size("yhi") * lax.axis_size("ylo")
    expert = (lax.axis_index("yhi") * lax.axis_size("core") + lax.axis_index("core")) * 2 + ylo
    token_count, model_width = tokens.shape

    gate_ups, pending_a, pending_b = expert_weights(w_gate, w_up, w_down, ylo)

    experts = jnp.arange(lax.axis_size("core") * chips, dtype=jnp.int32)
    weight = jnp.sum(
        jnp.where(expert_ids[:, :, None] == experts, gate_weights[:, :, None], 0.0), axis=1
    )
    high = lax.reduce_precision(weight, exponent_bits=8, mantissa_bits=7)
    low = weight - high
    packed = jnp.concatenate([high, low], axis=1).astype(jnp.bfloat16).T
    extra = packed.shape[0]
    packed = jnp.pad(packed, ((0, 0), (0, model_width - token_count)))
    mine, other = spread(jnp.concatenate([tokens, packed]), chips)
    both = jnp.concatenate([mine, other])
    rows = both[:, :token_count].reshape(-1, model_width)
    halves = jnp.swapaxes(both[:, token_count:, :token_count], 1, 2).astype(jnp.float32)
    table = (halves[..., : extra // 2] + halves[..., extra // 2 :]).reshape(-1, extra // 2)
    scale = lax.dynamic_index_in_dim(table, expert, axis=1, keepdims=True)

    gate_parts = [
        jnp.dot(rows, g[0].T, preferred_element_type=jnp.float32) for g in gate_ups
    ]
    late_rows, pending_a, pending_b = lax.optimization_barrier((rows, pending_a, pending_b))
    sets = [(g[0], g[1], d) for g, d in zip(gate_ups, finish_down(pending_a, pending_b))]
    hiddens = []
    for gate_part, weights in zip(gate_parts, sets):
        up_part = jnp.dot(late_rows, weights[1].T, preferred_element_type=jnp.float32)
        hidden = (jax.nn.silu(gate_part) * up_part).astype(jnp.bfloat16)
        hiddens.append(lax.optimization_barrier(hidden))

    def down(hiddens, first, last):
        out = None
        for hidden, weights in zip(hiddens, sets):
            part = jnp.dot(hidden[first:last], weights[2], preferred_element_type=jnp.float32)
            out = part if out is None else out + part
        weighted = out.astype(jnp.bfloat16).astype(jnp.float32) * scale[first:last]
        return weighted.reshape(chips, token_count, model_width)

    half = chips * token_count
    theirs = down(hiddens, half, 2 * half)
    hiddens, theirs = lax.optimization_barrier((hiddens, theirs))
    partner = lax.ppermute(theirs.astype(jnp.bfloat16), "core", perm=SWAP)
    partial = (down(hiddens, 0, half) + partner.astype(jnp.float32)).astype(jnp.bfloat16)
    back = lax.all_to_all(partial, CHIPS, split_axis=0, concat_axis=0, tiled=True)
    mixed = jnp.sum(back.astype(jnp.float32), axis=0)
    return mixed.astype(jnp.bfloat16)


def solution(mesh):
    grp, blk = mesh.devices.shape
    ylo = 2
    fine = Mesh(
        mesh.devices.reshape(2, grp // 2, 4, blk // (4 * ylo), ylo),
        ("yhi", "core", "x", "z", "ylo"),
    )
    rows = P(("yhi", "core", "x", "z", "ylo"), None)
    weights = P(("yhi", "core"), ("x", "z", "ylo"), None)
    return jax.shard_map(
        per_device,
        mesh=fine,
        in_specs=(rows, rows, rows, weights, weights, weights),
        out_specs=rows,
        check_vma=False,
    )
```

```python
import jax
import jax.numpy as jnp
from jax import lax
from jax.sharding import Mesh
from jax.sharding import PartitionSpec as P

CHIPS = ("yhi", "ylo")
SWAP = [(0, 1), (1, 0)]


AHEAD = [(i, (i + 1) % 4) for i in range(4)]
BEHIND = [(i, (i - 1) % 4) for i in range(4)]


def first_hop(value, axis):
    return lax.ppermute(value, axis, perm=AHEAD), lax.ppermute(value, axis, perm=BEHIND)


def far_hop(value, near, axis):
    from_minus, from_plus = near
    split = 0 if value.shape[0] % 2 == 0 else value.ndim - 1
    half = value.shape[split] // 2
    far = jnp.concatenate(
        [
            lax.ppermute(lax.slice_in_dim(from_minus, 0, half, axis=split), axis, perm=AHEAD),
            lax.ppermute(
                lax.slice_in_dim(from_plus, half, 2 * half, axis=split), axis, perm=BEHIND
            ),
        ],
        axis=split,
    )
    return jnp.stack([value, from_plus, far, from_minus])


def ring_of_four(value, axis):
    return far_hop(value, first_hop(value, axis), axis)


def expert_weights(w_gate, w_up, w_down, ylo):
    stacked = jnp.stack([w_gate, w_up, w_down], axis=1)
    rows = stacked.shape[2]
    padded = -(-rows // 16) * 16
    stacked = jnp.pad(stacked, ((0, 0), (0, 0), (0, padded - rows), (0, 0)))
    keep = lax.dynamic_index_in_dim(stacked, ylo, axis=0, keepdims=False)
    send = lax.dynamic_index_in_dim(stacked, 1 - ylo, axis=0, keepdims=False)
    got = lax.ppermute(send, "ylo", perm=SWAP)
    first_a = ring_of_four(keep, "z")
    first_b = ring_of_four(got, "x")
    first_a, first_b = lax.optimization_barrier((first_a, first_b))
    gate_up_a = ring_of_four(first_a[:, :2], "x")
    gate_up_b = ring_of_four(first_b[:, :2], "z")
    gate_up_a, gate_up_b, down_a, down_b = lax.optimization_barrier(
        (gate_up_a, gate_up_b, first_a[:, 2], first_b[:, 2])
    )
    width = stacked.shape[-1]
    gate_ups = [jnp.moveaxis(g, 2, 0).reshape(2, -1, width) for g in (gate_up_a, gate_up_b)]
    return gate_ups, (down_a, first_hop(down_a, "x")), (down_b, first_hop(down_b, "z"))


def finish_down(pending_a, pending_b):
    width = pending_a[0].shape[-1]
    return [
        far_hop(*pending_a, "x").reshape(-1, width),
        far_hop(*pending_b, "z").reshape(-1, width),
    ]


def spread(value, chips):
    sent = jnp.broadcast_to(value[None], (chips,) + value.shape)
    mine = lax.all_to_all(sent, CHIPS, split_axis=0, concat_axis=0, tiled=True)
    other = lax.ppermute(mine, "core", perm=SWAP)
    return mine, other


def per_device(tokens, expert_ids, gate_weights, w_gate, w_up, w_down):
    ylo = lax.axis_index("ylo")
    chips = lax.axis_size("yhi") * lax.axis_size("ylo")
    expert = (lax.axis_index("yhi") * lax.axis_size("core") + lax.axis_index("core")) * 2 + ylo
    token_count, model_width = tokens.shape

    gate_ups, pending_a, pending_b = expert_weights(w_gate, w_up, w_down, ylo)

    experts = jnp.arange(lax.axis_size("core") * chips, dtype=jnp.int32)
    weight = jnp.sum(
        jnp.where(expert_ids[:, :, None] == experts, gate_weights[:, :, None], 0.0), axis=1
    )
    high = lax.reduce_precision(weight, exponent_bits=8, mantissa_bits=7)
    low = weight - high
    packed = jnp.concatenate([high, low], axis=1).astype(jnp.bfloat16).T
    extra = packed.shape[0]
    packed = jnp.pad(packed, ((0, 0), (0, model_width - token_count)))
    mine, other = spread(jnp.concatenate([tokens, packed]), chips)
    both = jnp.concatenate([mine, other])
    rows = both[:, :token_count].reshape(-1, model_width)
    halves = jnp.swapaxes(both[:, token_count:, :token_count], 1, 2).astype(jnp.float32)
    table = (halves[..., : extra // 2] + halves[..., extra // 2 :]).reshape(-1, extra // 2)
    scale = lax.dynamic_index_in_dim(table, expert, axis=1, keepdims=True)

    gate_parts = [
        jnp.dot(rows, g[0].T, preferred_element_type=jnp.float32) for g in gate_ups
    ]
    late_rows, pending_a, pending_b = lax.optimization_barrier((rows, pending_a, pending_b))
    sets = [(g[0], g[1], d) for g, d in zip(gate_ups, finish_down(pending_a, pending_b))]
    hiddens = []
    for gate_part, weights in zip(gate_parts, sets):
        up_part = jnp.dot(late_rows, weights[1].T, preferred_element_type=jnp.float32)
        hidden = (jax.nn.silu(gate_part) * up_part).astype(jnp.bfloat16)
        hiddens.append(lax.optimization_barrier(hidden))

    def down(hiddens, first, last):
        out = None
        for hidden, weights in zip(hiddens, sets):
            part = jnp.dot(hidden[first:last], weights[2], preferred_element_type=jnp.float32)
            out = part if out is None else out + part
        weighted = out.astype(jnp.bfloat16).astype(jnp.float32) * scale[first:last]
        return weighted.reshape(chips, token_count, model_width)

    half = chips * token_count
    theirs = down(hiddens, half, 2 * half)
    hiddens, theirs = lax.optimization_barrier((hiddens, theirs))
    partner = lax.ppermute(theirs.astype(jnp.bfloat16), "core", perm=SWAP)
    partial = (down(hiddens, 0, half) + partner.astype(jnp.float32)).astype(jnp.bfloat16)
    back = lax.all_to_all(partial, CHIPS, split_axis=0, concat_axis=0, tiled=True)
    mixed = jnp.sum(back.astype(jnp.float32), axis=0)
    return mixed.astype(jnp.bfloat16)


def solution(mesh):
    grp, blk = mesh.devices.shape
    ylo = 2
    fine = Mesh(
        mesh.devices.reshape(2, grp // 2, 4, blk // (4 * ylo), ylo),
        ("yhi", "core", "x", "z", "ylo"),
    )
    rows = P(("yhi", "core", "x", "z", "ylo"), None)
    weights = P(("yhi", "core"), ("x", "z", "ylo"), None)
    return jax.shard_map(
        per_device,
        mesh=fine,
        in_specs=(rows, rows, rows, weights, weights, weights),
        out_specs=rows,
        check_vma=False,
    )
```

```python
import jax
import jax.numpy as jnp
from jax import lax
from jax.sharding import Mesh
from jax.sharding import PartitionSpec as P

CHIPS = ("yhi", "ylo")
SWAP = [(0, 1), (1, 0)]


AHEAD = [(i, (i + 1) % 4) for i in range(4)]
BEHIND = [(i, (i - 1) % 4) for i in range(4)]


def first_hop(value, axis):
    return lax.ppermute(value, axis, perm=AHEAD), lax.ppermute(value, axis, perm=BEHIND)


def far_hop(value, near, axis):
    from_minus, from_plus = near
    half = value.shape[-1] // 2
    far = jnp.concatenate(
        [
            lax.ppermute(from_minus[..., :half], axis, perm=AHEAD),
            lax.ppermute(from_plus[..., half:], axis, perm=BEHIND),
        ],
        axis=-1,
    )
    return jnp.stack([value, from_plus, far, from_minus])


def ring_of_four(value, axis):
    return far_hop(value, first_hop(value, axis), axis)


def expert_weights(w_gate, w_up, w_down, ylo):
    stacked = jnp.stack([w_gate, w_up, w_down], axis=1)
    rows = stacked.shape[2]
    padded = -(-rows // 16) * 16
    stacked = jnp.pad(stacked, ((0, 0), (0, 0), (0, padded - rows), (0, 0)))
    keep = lax.dynamic_index_in_dim(stacked, ylo, axis=0, keepdims=False)
    send = lax.dynamic_index_in_dim(stacked, 1 - ylo, axis=0, keepdims=False)
    got = lax.ppermute(send, "ylo", perm=SWAP)
    first_a = ring_of_four(keep, "z")
    first_b = ring_of_four(got, "x")
    first_a, first_b = lax.optimization_barrier((first_a, first_b))
    gate_up_a = ring_of_four(first_a[:, :2], "x")
    gate_up_b = ring_of_four(first_b[:, :2], "z")
    gate_up_a, gate_up_b, down_a, down_b = lax.optimization_barrier(
        (gate_up_a, gate_up_b, first_a[:, 2], first_b[:, 2])
    )
    width = stacked.shape[-1]
    gate_ups = [jnp.moveaxis(g, 2, 0).reshape(2, -1, width) for g in (gate_up_a, gate_up_b)]
    return gate_ups, (down_a, first_hop(down_a, "x")), (down_b, first_hop(down_b, "z"))


def finish_down(pending_a, pending_b):
    width = pending_a[0].shape[-1]
    return [
        far_hop(*pending_a, "x").reshape(-1, width),
        far_hop(*pending_b, "z").reshape(-1, width),
    ]


def spread(value, chips):
    del chips
    mine = lax.all_gather(value, CHIPS, axis=0, tiled=False)
    other = lax.ppermute(mine, "core", perm=SWAP)
    return mine, other


def per_device(tokens, expert_ids, gate_weights, w_gate, w_up, w_down):
    ylo = lax.axis_index("ylo")
    chips = lax.axis_size("yhi") * lax.axis_size("ylo")
    expert = (lax.axis_index("yhi") * lax.axis_size("core") + lax.axis_index("core")) * 2 + ylo
    token_count, model_width = tokens.shape

    gate_ups, pending_a, pending_b = expert_weights(w_gate, w_up, w_down, ylo)

    experts = jnp.arange(lax.axis_size("core") * chips, dtype=jnp.int32)
    weight = jnp.sum(
        jnp.where(expert_ids[:, :, None] == experts, gate_weights[:, :, None], 0.0), axis=1
    )
    high = lax.reduce_precision(weight, exponent_bits=8, mantissa_bits=7)
    low = weight - high
    packed = jnp.concatenate([high, low], axis=1).astype(jnp.bfloat16).T
    extra = packed.shape[0]
    packed = jnp.pad(packed, ((0, 0), (0, model_width - token_count)))
    mine, other = spread(jnp.concatenate([tokens, packed]), chips)
    both = jnp.concatenate([mine, other])
    rows = both[:, :token_count].reshape(-1, model_width)
    halves = jnp.swapaxes(both[:, token_count:, :token_count], 1, 2).astype(jnp.float32)
    table = (halves[..., : extra // 2] + halves[..., extra // 2 :]).reshape(-1, extra // 2)
    scale = lax.dynamic_index_in_dim(table, expert, axis=1, keepdims=True)

    gate_parts = [
        jnp.dot(rows, g[0].T, preferred_element_type=jnp.float32) for g in gate_ups
    ]
    late_rows, pending_a, pending_b = lax.optimization_barrier((rows, pending_a, pending_b))
    sets = [(g[0], g[1], d) for g, d in zip(gate_ups, finish_down(pending_a, pending_b))]
    hiddens = []
    for gate_part, weights in zip(gate_parts, sets):
        up_part = jnp.dot(late_rows, weights[1].T, preferred_element_type=jnp.float32)
        hidden = (jax.nn.silu(gate_part) * up_part).astype(jnp.bfloat16)
        hiddens.append(lax.optimization_barrier(hidden))

    def down(hiddens, first, last):
        out = None
        for hidden, weights in zip(hiddens, sets):
            part = jnp.dot(hidden[first:last], weights[2], preferred_element_type=jnp.float32)
            out = part if out is None else out + part
        weighted = out.astype(jnp.bfloat16).astype(jnp.float32) * scale[first:last]
        return weighted.reshape(chips, token_count, model_width)

    half = chips * token_count
    theirs = down(hiddens, half, 2 * half)
    hiddens, theirs = lax.optimization_barrier((hiddens, theirs))
    partner = lax.ppermute(theirs.astype(jnp.bfloat16), "core", perm=SWAP)
    partial = (down(hiddens, 0, half) + partner.astype(jnp.float32)).astype(jnp.bfloat16)
    back = lax.all_to_all(partial, CHIPS, split_axis=0, concat_axis=0, tiled=True)
    mixed = jnp.sum(back.astype(jnp.float32), axis=0)
    return mixed.astype(jnp.bfloat16)


def solution(mesh):
    grp, blk = mesh.devices.shape
    ylo = 2
    fine = Mesh(
        mesh.devices.reshape(2, grp // 2, 4, blk // (4 * ylo), ylo),
        ("yhi", "core", "x", "z", "ylo"),
    )
    rows = P(("yhi", "core", "x", "z", "ylo"), None)
    weights = P(("yhi", "core"), ("x", "z", "ylo"), None)
    return jax.shard_map(
        per_device,
        mesh=fine,
        in_specs=(rows, rows, rows, weights, weights, weights),
        out_specs=rows,
        check_vma=False,
    )
```

```python
import jax
import jax.numpy as jnp
from jax import lax
from jax.sharding import Mesh
from jax.sharding import PartitionSpec as P

CHIPS = ("yhi", "ylo")
SWAP = [(0, 1), (1, 0)]


AHEAD = [(i, (i + 1) % 4) for i in range(4)]
BEHIND = [(i, (i - 1) % 4) for i in range(4)]


def first_hop(value, axis):
    return lax.ppermute(value, axis, perm=AHEAD), lax.ppermute(value, axis, perm=BEHIND)


def far_pieces(value, near, axis):
    from_minus, from_plus = near
    half = value.shape[-1] // 2
    far = jnp.concatenate(
        [
            lax.ppermute(from_minus[..., :half], axis, perm=AHEAD),
            lax.ppermute(from_plus[..., half:], axis, perm=BEHIND),
        ],
        axis=-1,
    )
    return (value, from_plus, far, from_minus)


def far_hop(value, near, axis):
    return jnp.stack(far_pieces(value, near, axis))


def ring_of_four(value, axis):
    return far_hop(value, first_hop(value, axis), axis)


def expert_weights(w_gate, w_up, w_down, ylo):
    stacked = jnp.stack([w_gate, w_up, w_down], axis=1)
    rows = stacked.shape[2]
    padded = -(-rows // 16) * 16
    stacked = jnp.pad(stacked, ((0, 0), (0, 0), (0, padded - rows), (0, 0)))
    keep = lax.dynamic_index_in_dim(stacked, ylo, axis=0, keepdims=False)
    send = lax.dynamic_index_in_dim(stacked, 1 - ylo, axis=0, keepdims=False)
    got = lax.ppermute(send, "ylo", perm=SWAP)
    first_a = ring_of_four(keep, "z")
    first_b = ring_of_four(got, "x")
    first_a, first_b = lax.optimization_barrier((first_a, first_b))
    lead_a, lead_b = first_a[:, :2], first_b[:, :2]
    gate_up_a = far_pieces(lead_a, first_hop(lead_a, "x"), "x")
    gate_up_b = far_pieces(lead_b, first_hop(lead_b, "z"), "z")
    gate_up_a, gate_up_b, down_a, down_b = lax.optimization_barrier(
        (gate_up_a, gate_up_b, first_a[:, 2], first_b[:, 2])
    )
    gate_up_a, gate_up_b = jnp.stack(gate_up_a), jnp.stack(gate_up_b)
    width = stacked.shape[-1]
    gate_ups = [jnp.moveaxis(g, 2, 0).reshape(2, -1, width) for g in (gate_up_a, gate_up_b)]
    return gate_ups, (down_a, first_hop(down_a, "x")), (down_b, first_hop(down_b, "z"))


def finish_down(pending_a, pending_b):
    width = pending_a[0].shape[-1]
    return [
        far_hop(*pending_a, "x").reshape(-1, width),
        far_hop(*pending_b, "z").reshape(-1, width),
    ]


def spread(value, chips):
    sent = jnp.broadcast_to(value[None], (chips,) + value.shape)
    mine = lax.all_to_all(sent, CHIPS, split_axis=0, concat_axis=0, tiled=True)
    other = lax.ppermute(mine, "core", perm=SWAP)
    return mine, other


def per_device(tokens, expert_ids, gate_weights, w_gate, w_up, w_down):
    ylo = lax.axis_index("ylo")
    chips = lax.axis_size("yhi") * lax.axis_size("ylo")
    expert = (lax.axis_index("yhi") * lax.axis_size("core") + lax.axis_index("core")) * 2 + ylo
    token_count, model_width = tokens.shape

    gate_ups, pending_a, pending_b = expert_weights(w_gate, w_up, w_down, ylo)

    experts = jnp.arange(lax.axis_size("core") * chips, dtype=jnp.int32)
    weight = jnp.sum(
        jnp.where(expert_ids[:, :, None] == experts, gate_weights[:, :, None], 0.0), axis=1
    )
    high = lax.reduce_precision(weight, exponent_bits=8, mantissa_bits=7)
    low = weight - high
    packed = jnp.concatenate([high, low], axis=1).astype(jnp.bfloat16).T
    extra = packed.shape[0]
    packed = jnp.pad(packed, ((0, 0), (0, model_width - token_count)))
    mine, other = spread(jnp.concatenate([tokens, packed]), chips)
    both = jnp.concatenate([mine, other])
    rows = both[:, :token_count].reshape(-1, model_width)
    halves = jnp.swapaxes(both[:, token_count:, :token_count], 1, 2).astype(jnp.float32)
    table = (halves[..., : extra // 2] + halves[..., extra // 2 :]).reshape(-1, extra // 2)
    scale = lax.dynamic_index_in_dim(table, expert, axis=1, keepdims=True)

    gate_parts = [
        jnp.dot(rows, g[0].T, preferred_element_type=jnp.float32) for g in gate_ups
    ]
    late_rows, pending_a, pending_b = lax.optimization_barrier((rows, pending_a, pending_b))
    sets = [(g[0], g[1], d) for g, d in zip(gate_ups, finish_down(pending_a, pending_b))]
    hiddens = []
    for gate_part, weights in zip(gate_parts, sets):
        up_part = jnp.dot(late_rows, weights[1].T, preferred_element_type=jnp.float32)
        hidden = (jax.nn.silu(gate_part) * up_part).astype(jnp.bfloat16)
        hiddens.append(lax.optimization_barrier(hidden))

    def down(hiddens, first, last):
        out = None
        for hidden, weights in zip(hiddens, sets):
            part = jnp.dot(hidden[first:last], weights[2], preferred_element_type=jnp.float32)
            out = part if out is None else out + part
        weighted = out.astype(jnp.bfloat16).astype(jnp.float32) * scale[first:last]
        return weighted.reshape(chips, token_count, model_width)

    half = chips * token_count
    theirs = down(hiddens, half, 2 * half)
    hiddens, theirs = lax.optimization_barrier((hiddens, theirs))
    partner = lax.ppermute(theirs.astype(jnp.bfloat16), "core", perm=SWAP)
    partial = (down(hiddens, 0, half) + partner.astype(jnp.float32)).astype(jnp.bfloat16)
    back = lax.all_to_all(partial, CHIPS, split_axis=0, concat_axis=0, tiled=True)
    mixed = jnp.sum(back.astype(jnp.float32), axis=0)
    return mixed.astype(jnp.bfloat16)


def solution(mesh):
    grp, blk = mesh.devices.shape
    ylo = 2
    fine = Mesh(
        mesh.devices.reshape(2, grp // 2, 4, blk // (4 * ylo), ylo),
        ("yhi", "core", "x", "z", "ylo"),
    )
    rows = P(("yhi", "core", "x", "z", "ylo"), None)
    weights = P(("yhi", "core"), ("x", "z", "ylo"), None)
    return jax.shard_map(
        per_device,
        mesh=fine,
        in_specs=(rows, rows, rows, weights, weights, weights),
        out_specs=rows,
        check_vma=False,
    )
```
